256 devices in a mesh: region: 256 (over z, x, y, core).
Axes of the slice: x: 4, y: 4, z: 8, core: 2. Of those that a mesh axis runs over, the one named last changes fastest.
Arguments:
- features: bfloat16 [8, 131072, 256], P(None, 'region'), may hold values from -6 to 6
- line_mask: int32 [131072, 512], P('region'), may hold values 0 or 1
- send_rows: int32 [1024, 128], P('region'), may hold values from 0 to 511
- attach_rows: int32 [1024, 128], P('region'), may hold values from 0 to 511
- tile_count: int32 [1024], P('region'), may hold values from 32 to 128, as said below
- self_weight: bfloat16 [2, 256, 256], replicated, may hold values from -0.375 to 0.375
- neigh_weight: bfloat16 [2, 256, 256], replicated, may hold values from -0.375 to 0.375
- layer_bias: float32 [2, 256], replicated, may hold values from -3 to 3
- readout: bfloat16 [2, 256], replicated, may hold values from -0.375 to 0.375
- load_table: float32 [16, 2, 131072], P(None, None, 'region')
- scenario_profile: int32 [8], replicated, may hold values from 0 to 15
- diag_admit: float32 [131072], P('region'), may hold values from 6 to 10
- conductance: float32 [131072], P('region'), may hold values from 0.5 to 1.5
- susceptance: float32 [131072], P('region'), may hold values from -3 to -1
- load_coeff: float32 [131072], P('region'), may hold values from 0.5 to 2.5
- region_inverse: bfloat16 [262144, 1024], P('region')
Outputs:
- voltage: float32 [8, 2, 131072], P(None, None, 'region')
The draws below stay inside these ranges and needn't reach their ends.
Inputs may be any that keep to these rules, and one draw needn't show every extreme that they name: `tile_count`: rows of a tile at or beyond its count are padding and carry nothing; counts are uneven across tiles.
All inputs are finite; a program needn't handle non-finite values. No bound on the sum of `line_mask` on one device may be relied on, other than what follows from the above.
Results may differ from the reference program's by a relative error of at most 0.023.
Values may be sent and summed in bfloat16 or wider, within the bound.
No kernel may reach another device: no remote copies, remote signals or barrier semaphores. Data moves between devices by JAX's collectives and lax.ppermute only.
A program may use at most 128 MiB of HBM per device.

```python
import math
import jax
import jax.numpy as jnp
from jax import lax

B = 512
S = 8
H = 256
P_SIZE = 128
K = 4
RW = 16
LAYERS = 2
NEWTON = 2
SWEEPS = 3
NPROF = 16
NB = 131072
NK = 1024
ORDER = 1024
N_REGION = 256


def draw_tile_count(key, part):
    streams = jax.random.split(key, 4)
    factor_one = jax.random.randint(streams[0], (NK,), 0, P_SIZE)
    factor_two = jax.random.randint(streams[1], (NK,), 0, P_SIZE)
    counts = P_SIZE - 3 * factor_one * factor_two // (4 * P_SIZE)
    highest_slot = jax.random.randint(streams[2], (), 0, NK)
    lowest_slot = (highest_slot + 1 + jax.random.randint(streams[3], (), 0, NK - 1)) % NK
    positions = jnp.arange(NK)
    counts = jnp.where(positions == highest_slot, P_SIZE, counts)
    counts = jnp.where(positions == lowest_slot, P_SIZE // 4, counts)
    return counts.astype(jnp.int32)


def draw_load_table(key, part):
    streams = jax.random.split(key, 2)
    extent = (NPROF, 2, NB)
    position = jnp.arange(NB, dtype=jnp.float32)[None, None, :]
    rising = 1.0 + 2.0 * position / (NB - 1)
    spread = jnp.exp(jax.random.uniform(streams[0], (1, 1, NB), minval=0.0, maxval=math.log(10.0)))
    basis = jax.random.normal(streams[1], extent)
    return (2.0 * rising * spread * basis).astype(jnp.float32)


def draw_region_inverse(key, part):
    streams = jax.random.split(key, 2)
    extent = (2 * NB, ORDER)
    row_index = jnp.arange(2 * NB, dtype=jnp.int32)[:, None] % ORDER
    column = jnp.arange(ORDER, dtype=jnp.int32)[None, :]
    spread_off = jax.random.normal(streams[0], extent)
    diagonal_value = jax.random.uniform(streams[1], (2 * NB, 1), minval=0.12, maxval=0.24)
    matrix = spread_off * (0.06 / math.sqrt(ORDER)) + jnp.where(row_index == column, diagonal_value, 0.0)
    return matrix.astype(jnp.bfloat16)


def set_ends(result, stream_key, least, top_value):
    longest = result.shape.index(max(result.shape))
    spots = []
    for shift in (0, 1):
        where = [jax.random.randint(jax.random.fold_in(stream_key, axis), (), 0, length) for axis, length in enumerate(result.shape)]
        where[longest] = (where[longest] + shift) % result.shape[longest]
        spots.append(tuple(where))
    return result.at[spots[0]].set(least).at[spots[1]].set(top_value)


def levels(stream_key, shape, pieces, least, top_value):
    def one(dim, blocks):
        draws = jax.random.uniform(jax.random.fold_in(jax.random.fold_in(stream_key, 6), dim), (blocks,), jnp.float32, least / len(pieces), top_value / len(pieces))
        return jnp.repeat(jnp.exp(draws), shape[dim] // blocks).reshape((-1,) + (1,) * (len(shape) - dim - 1))

    factor_of = one(*pieces[0])
    for cut in pieces[1:]:
        factor_of = factor_of * one(*cut)
    return factor_of


def centred(key, shape, scale, bound, cuts=(), held_as=jnp.bfloat16):
    loudness = levels(key, shape, cuts, -0.22, 0.18) if cuts else 1.0
    values = jax.random.normal(key, shape, jnp.float32) * scale * loudness
    return jnp.minimum(jnp.maximum(values, -bound), bound).astype(held_as)


def setup_inputs(seed: int = 0) -> dict:
    key_list = jax.random.split(jax.random.key(seed), 17)
    return {
        "features": centred(key_list[0], (S, NB, H), 1.0, 6.0, ((1, 256),)),
        "line_mask": set_ends((jax.random.randint(key_list[1], (NB, B), 0, B) < 4).astype(jnp.int32), jax.random.fold_in(key_list[1], 1), 0, 1),
        "send_rows": set_ends(jax.random.randint(key_list[2], (NK, P_SIZE), 0, B), jax.random.fold_in(key_list[2], 1), 0, B - 1).astype(jnp.int32),
        "attach_rows": set_ends(jax.random.randint(key_list[3], (NK, P_SIZE), 0, B), jax.random.fold_in(key_list[3], 1), 0, B - 1).astype(jnp.int32),
        "tile_count": draw_tile_count(jax.random.fold_in(key_list[16], 71), 0),
        "self_weight": centred(key_list[5], (LAYERS, H, H), H ** -0.5, 0.375),
        "neigh_weight": centred(key_list[6], (LAYERS, H, H), H ** -0.5, 0.375),
        "layer_bias": centred(key_list[7], (LAYERS, H), 0.5, 3.0, (), jnp.float32),
        "readout": centred(key_list[8], (2, H), H ** -0.5, 0.375),
        "load_table": draw_load_table(jax.random.fold_in(key_list[16], 71), 0),
        "scenario_profile": set_ends(jax.random.randint(key_list[10], (S,), 0, NPROF), jax.random.fold_in(key_list[10], 1), 0, NPROF - 1).astype(jnp.int32),
        "diag_admit": jnp.clip(6.0 + 4.0 * jax.random.uniform(key_list[11], (NB,), jnp.float32) ** levels(key_list[11], (NB,), ((0, 256),), -0.2, 0.2), 6.0, 10.0),
        "conductance": jnp.clip(0.5 + 1.0 * jax.random.uniform(key_list[12], (NB,), jnp.float32) ** levels(key_list[12], (NB,), ((0, 256),), -0.2, 0.2), 0.5, 1.5),
        "susceptance": jnp.clip(-3.0 + 2.0 * jax.random.uniform(key_list[13], (NB,), jnp.float32) ** levels(key_list[13], (NB,), ((0, 256),), -0.2, 0.2), -3.0, -1.0),
        "load_coeff": jnp.clip(0.5 + 2.0 * jax.random.uniform(key_list[14], (NB,), jnp.float32) ** levels(key_list[14], (NB,), ((0, 256),), -0.2, 0.2), 0.5, 2.5),
        "region_inverse": draw_region_inverse(jax.random.fold_in(key_list[16], 71), 0),
    }


trust_radius = 8.0
highest = lax.Precision.HIGHEST

def shift_regions(values, offset):
    if offset > 0:
        return jnp.concatenate([jnp.zeros_like(values[:offset]), values[:-offset]], axis=0)
    return jnp.concatenate([values[-offset:], jnp.zeros_like(values[:-offset])], axis=0)

def rotate(conduct, suscept, beside, axis):
    real_part = jnp.take(beside, 0, axis=axis)
    imag_part = jnp.take(beside, 1, axis=axis)
    return jnp.stack([conduct * real_part - suscept * imag_part, suscept * real_part + conduct * imag_part], axis=axis)

def reference(features, line_mask, send_rows, attach_rows, tile_count, self_weight, neigh_weight, layer_bias, readout, load_table, scenario_profile, diag_admit, conductance, susceptance, load_coeff, region_inverse):
    regions = N_REGION
    offsets = (1, -1, RW, -RW)
    senders = send_rows.reshape(regions, K * P_SIZE)
    attach = attach_rows.reshape(regions, K * P_SIZE)
    live_rows = (jnp.arange(P_SIZE, dtype=jnp.int32)[None, None, :] < tile_count.reshape(regions, K)[:, :, None]).reshape(regions, K * P_SIZE)
    line_masks = line_mask.reshape(regions, B, B)
    hidden = jnp.moveaxis(features.reshape(S, regions, B, H), 1, 0)
    bus_iota = jnp.arange(B, dtype=jnp.int32)
    for number in range(LAYERS):
        tile_rows = jax.vmap(lambda rows, indices: jnp.take(rows, indices, axis=1))(hidden, senders)
        tile_rows = jnp.where(live_rows[:, None, :, None], tile_rows, jnp.zeros((), hidden.dtype))
        tile_rows = tile_rows.reshape(regions, S, K, P_SIZE, H)
        incoming = jnp.stack([shift_regions(tile_rows[:, :, slot_index], offsets[slot_index]) for slot_index in range(K)], axis=2)
        incoming = incoming.reshape(regions, S, K * P_SIZE, H)
        weight_self = self_weight[number].astype(jnp.float32)
        weight_neigh = neigh_weight[number].astype(jnp.float32)
        offset_bias = layer_bias[number]

        def one_layer(inputs, weight_self=weight_self, weight_neigh=weight_neigh, offset_bias=offset_bias):
            rows, region_mask, arrived, attached = inputs
            matches = (attached[:, None] == bus_iota[None, :]).astype(jnp.float32)
            inside = jnp.einsum('ij,sjh->sih', region_mask.astype(jnp.float32), rows.astype(jnp.float32))
            border = jnp.einsum('jb,sjh->sbh', matches, arrived.astype(jnp.float32))
            gathered = (0.25 * (inside + border)).astype(jnp.bfloat16)
            summed = jnp.einsum('sbh,hk->sbk', rows.astype(jnp.float32), weight_self)
            summed = summed + jnp.einsum('sbh,hk->sbk', gathered.astype(jnp.float32), weight_neigh) + offset_bias
            return (rows.astype(jnp.float32) + jax.nn.silu(summed)).astype(jnp.bfloat16)
        hidden = lax.map(one_layer, (hidden, line_masks, incoming, attach))
    flat_start = jnp.array([1.0, 0.0], dtype=jnp.float32)[None, None, :, None]
    readout_full = readout.astype(jnp.float32)
    voltage = lax.map(lambda rows: jnp.einsum('sbh,ch->scb', rows.astype(jnp.float32), readout_full), hidden) + flat_start
    choose = (scenario_profile[:, None] == jnp.arange(NPROF, dtype=jnp.int32)[None, :]).astype(jnp.float32)
    injection = jnp.einsum('sp,pcn->scn', choose, load_table, precision=highest)
    injection = jnp.transpose(injection.reshape(S, 2, regions, B), (2, 0, 1, 3))
    diagonal = diag_admit.reshape(regions, 1, 1, B)
    load_rows = load_coeff.reshape(regions, 1, 1, B)
    conduct_rows = conductance.reshape(regions, 1, B)
    suscept_rows = susceptance.reshape(regions, 1, B)
    inverses = region_inverse.reshape(regions, 2 * B, 2 * B)

    def boundary(values):
        tile_rows = jax.vmap(lambda rows, indices: jnp.take(rows, indices, axis=2))(values, senders)
        tile_rows = jnp.where(live_rows[:, None, None, :], tile_rows, jnp.zeros((), values.dtype))
        tile_rows = tile_rows.reshape(regions, S, 2, K, P_SIZE)
        incoming = jnp.stack([shift_regions(tile_rows[:, :, :, slot_index], offsets[slot_index]) for slot_index in range(K)], axis=3)
        incoming = incoming.reshape(regions, S, 2, K * P_SIZE)

        def spread(inputs):
            arrived, attached = inputs
            matches = (attached[:, None] == bus_iota[None, :]).astype(values.dtype)
            return jnp.einsum('scj,jb->scb', arrived, matches, precision=highest)
        return lax.map(spread, (incoming, attach))

    def mismatch(values):
        inside = lax.map(lambda pair: jnp.einsum('ij,scj->sci', pair[0].astype(values.dtype), pair[1], precision=highest), (line_masks, values))
        beside = inside + boundary(values)
        magnitude = values[:, :, 0:1] ** 2 + values[:, :, 1:2] ** 2
        return diagonal * values - rotate(conduct_rows, suscept_rows, beside, 2) + load_rows * magnitude * values - injection
    for newton in range(NEWTON):
        residual = mismatch(voltage)
        squares = lax.optimization_barrier(jnp.sum(residual * residual, axis=(0, 2, 3)))
        damping = jnp.minimum(1.0, trust_radius / jnp.sqrt(squares / (2 * B * regions) + 1e-06))
        update = jnp.zeros_like(voltage)
        for sweep_number in range(SWEEPS):
            forcing = -residual
            if sweep_number > 0:
                forcing = forcing + rotate(conduct_rows, suscept_rows, boundary(update), 2)
            forcing = forcing.reshape(regions, S, 2 * B).astype(jnp.bfloat16)
            update = lax.map(lambda pair: jnp.dot(pair[0], pair[1], preferred_element_type=jnp.float32), (forcing, inverses))
            update = update.reshape(regions, S, 2, B)
        voltage = voltage + damping[None, :, None, None] * update
    return jnp.transpose(voltage, (1, 2, 0, 3)).reshape(S, 2, regions * B)
```

```python
import jax
import jax.numpy as jnp
from jax import lax
from jax.sharding import PartitionSpec as P

RW = 16
NEWTON = 2
SWEEPS = 3


trust_radius = 8.0
highest = lax.Precision.HIGHEST


def from_behind(value, axis, steps):
    count = lax.axis_size(axis)
    first, last = (max(0, -steps), min(count, count - steps))
    return lax.ppermute(value, axis, [(source, source + steps) for source in range(first, last)])


def all_sum(value, axis):
    count = lax.axis_size(axis)
    if count & (count - 1):
        return lax.psum(value, axis)
    bit = 1
    while bit < count:
        value = value + lax.ppermute(value, axis, [(i, i ^ bit) for i in range(count)])
        bit *= 2
    return value


def rotate(conduct, suscept, beside, axis):
    real_part = jnp.take(beside, 0, axis=axis)
    imag_part = jnp.take(beside, 1, axis=axis)
    return jnp.stack(
        [conduct * real_part - suscept * imag_part, suscept * real_part + conduct * imag_part],
        axis=axis,
    )


def local(
    features,
    line_mask,
    send_rows,
    attach_rows,
    tile_count,
    self_weight,
    neigh_weight,
    layer_bias,
    readout,
    load_table,
    scenario_profile,
    diag_admit,
    conductance,
    susceptance,
    load_coeff,
    region_inverse,
):
    scenarios, buses, width = features.shape
    neighbours, tile_size = send_rows.shape
    offsets = (1, -1, RW, -RW)
    bus_iota = lax.broadcasted_iota(jnp.int32, (neighbours, tile_size, buses), 2)
    live = lax.broadcasted_iota(jnp.int32, (neighbours, tile_size), 1) < tile_count[:, None]
    pick = (send_rows[:, :, None] == bus_iota) & live[:, :, None]
    place = attach_rows[:, :, None] == bus_iota
    pick_half, pick_full = pick.astype(jnp.bfloat16), pick.astype(jnp.float32)
    place_half, place_full = place.astype(jnp.bfloat16), place.astype(jnp.float32)
    mask_half = line_mask.astype(jnp.bfloat16)
    mask_full = line_mask.astype(jnp.float32)

    def exchange(tiles):
        return jnp.stack(
            [from_behind(tiles[k], "region", offsets[k]) for k in range(neighbours)]
        )

    hidden = features
    for number in range(self_weight.shape[0]):
        tiles = jnp.einsum(
            "ktb,sbh->ksth", pick_half, hidden, preferred_element_type=jnp.float32
        ).astype(jnp.bfloat16)
        incoming = exchange(tiles)
        inside = jnp.einsum("ij,sjh->sih", mask_half, hidden, preferred_element_type=jnp.float32)
        own = jnp.einsum(
            "sbh,hk->sbk", hidden, self_weight[number], preferred_element_type=jnp.float32
        )
        border = jnp.einsum(
            "ktb,ksth->sbh", place_half, incoming, preferred_element_type=jnp.float32
        )
        gathered = (0.25 * (inside + border)).astype(jnp.bfloat16)
        summed = (
            own
            + jnp.einsum(
                "sbh,hk->sbk", gathered, neigh_weight[number], preferred_element_type=jnp.float32
            )
            + layer_bias[number]
        )
        hidden = (hidden.astype(jnp.float32) + jax.nn.silu(summed)).astype(jnp.bfloat16)
    flat_start = jnp.array([1.0, 0.0], dtype=jnp.float32)[None, :, None]
    voltage = (
        jnp.einsum("sbh,ch->scb", hidden, readout, preferred_element_type=jnp.float32) + flat_start
    )
    choose = (
        scenario_profile[:, None]
        == lax.broadcasted_iota(jnp.int32, (scenarios, load_table.shape[0]), 1)
    ).astype(jnp.float32)
    injection = jnp.einsum("sp,pcb->scb", choose, load_table, precision=highest)
    bus_total = buses * lax.axis_size("region")

    def halo(values):
        tiles = jnp.einsum("ktb,scb->ksct", pick_full, values, precision=highest)
        incoming = exchange(tiles)
        return jnp.einsum("ksct,ktb->scb", incoming, place_full, precision=highest)

    def inside_sum(values):
        return jnp.einsum("ij,scj->sci", mask_full, values, precision=highest)

    beside = inside_sum(voltage) + halo(voltage)
    for newton in range(NEWTON):
        magnitude = voltage[:, 0:1] ** 2 + voltage[:, 1:2] ** 2
        residual = (
            diag_admit * voltage
            - rotate(conductance, susceptance, beside, 1)
            + load_coeff * magnitude * voltage
            - injection
        )
        squares = all_sum(jnp.sum(residual * residual, axis=(1, 2)), "region")
        damping = jnp.minimum(1.0, trust_radius / jnp.sqrt(squares / (2 * bus_total) + 1e-06))
        update = jnp.zeros_like(voltage)
        for sweep_number in range(SWEEPS):
            forcing = -residual
            if sweep_number > 0:
                forcing = forcing + rotate(conductance, susceptance, halo(update), 1)
            forcing = forcing.reshape(scenarios, 2 * buses).astype(jnp.bfloat16)
            update = jnp.dot(forcing, region_inverse, preferred_element_type=jnp.float32).reshape(
                scenarios, 2, buses
            )
        step = damping[:, None, None]
        voltage = voltage + step * update
        if newton + 1 < NEWTON:
            beside = beside + step * (inside_sum(update) + halo(update))
    return voltage


def solution(mesh):
    in_specs = (
        P(None, "region", None),
        P("region", None),
        P("region", None),
        P("region", None),
        P("region"),
        P(),
        P(),
        P(),
        P(),
        P(None, None, "region"),
        P(),
        P("region"),
        P("region"),
        P("region"),
        P("region"),
        P("region", None),
    )
    out_specs = P(None, None, "region")
    return jax.shard_map(local, mesh=mesh, in_specs=in_specs, out_specs=out_specs, check_vma=False)
```

```python
import jax
import jax.numpy as jnp
from jax import lax
from jax.sharding import PartitionSpec as P

RW = 16
NEWTON = 2
SWEEPS = 3


trust_radius = 8.0
highest = lax.Precision.HIGHEST


def from_behind(value, axis, steps):
    count = lax.axis_size(axis)
    first, last = (max(0, -steps), min(count, count - steps))
    return lax.ppermute(value, axis, [(source, source + steps) for source in range(first, last)])


def sum_bits(axis):
    count = lax.axis_size(axis)
    if count & (count - 1):
        return None
    return [1 << b for b in range(count.bit_length() - 1)]


def sum_rounds(value, axis, bits):
    count = lax.axis_size(axis)
    for bit in bits:
        value = value + lax.ppermute(value, axis, [(i, i ^ bit) for i in range(count)])
    return value


def split_even(items, parts):
    cuts = [len(items) * p // parts for p in range(parts + 1)]
    return [items[cuts[p] : cuts[p + 1]] for p in range(parts)]


def rotate(conduct, suscept, beside, axis):
    real_part = jnp.take(beside, 0, axis=axis)
    imag_part = jnp.take(beside, 1, axis=axis)
    return jnp.stack(
        [conduct * real_part - suscept * imag_part, suscept * real_part + conduct * imag_part],
        axis=axis,
    )


def local(
    features,
    line_mask,
    send_rows,
    attach_rows,
    tile_count,
    self_weight,
    neigh_weight,
    layer_bias,
    readout,
    load_table,
    scenario_profile,
    diag_admit,
    conductance,
    susceptance,
    load_coeff,
    region_inverse,
):
    scenarios, buses, width = features.shape
    neighbours, tile_size = send_rows.shape
    offsets = (1, -1, RW, -RW)
    bus_iota = lax.broadcasted_iota(jnp.int32, (neighbours, tile_size, buses), 2)
    live = lax.broadcasted_iota(jnp.int32, (neighbours, tile_size), 1) < tile_count[:, None]
    pick = (send_rows[:, :, None] == bus_iota) & live[:, :, None]
    place = attach_rows[:, :, None] == bus_iota
    pick_half, pick_full = pick.astype(jnp.bfloat16), pick.astype(jnp.float32)
    place_half, place_full = place.astype(jnp.bfloat16), place.astype(jnp.float32)
    mask_half = line_mask.astype(jnp.bfloat16)
    mask_full = line_mask.astype(jnp.float32)

    def exchange(tiles):
        return jnp.stack(
            [from_behind(tiles[k], "region", offsets[k]) for k in range(neighbours)]
        )

    hidden = features
    for number in range(self_weight.shape[0]):
        tiles = jnp.einsum(
            "ktb,sbh->ksth", pick_half, hidden, preferred_element_type=jnp.float32
        ).astype(jnp.bfloat16)
        incoming = exchange(tiles)
        inside = jnp.einsum("ij,sjh->sih", mask_half, hidden, preferred_element_type=jnp.float32)
        own = jnp.einsum(
            "sbh,hk->sbk", hidden, self_weight[number], preferred_element_type=jnp.float32
        )
        border = jnp.einsum(
            "ktb,ksth->sbh", place_half, incoming, preferred_element_type=jnp.float32
        )
        gathered = (0.25 * (inside + border)).astype(jnp.bfloat16)
        summed = (
            own
            + jnp.einsum(
                "sbh,hk->sbk", gathered, neigh_weight[number], preferred_element_type=jnp.float32
            )
            + layer_bias[number]
        )
        hidden = (hidden.astype(jnp.float32) + jax.nn.silu(summed)).astype(jnp.bfloat16)
    flat_start = jnp.array([1.0, 0.0], dtype=jnp.float32)[None, :, None]
    voltage = (
        jnp.einsum("sbh,ch->scb", hidden, readout, preferred_element_type=jnp.float32) + flat_start
    )
    choose = (
        scenario_profile[:, None]
        == lax.broadcasted_iota(jnp.int32, (scenarios, load_table.shape[0]), 1)
    ).astype(jnp.float32)
    injection = jnp.einsum("sp,pcb->scb", choose, load_table, precision=highest)
    bus_total = buses * lax.axis_size("region")

    def halo(values):
        tiles = jnp.einsum("ktb,scb->ksct", pick_full, values, precision=highest)
        incoming = exchange(tiles)
        return jnp.einsum("ksct,ktb->scb", incoming, place_full, precision=highest)

    def inside_sum(values):
        return jnp.einsum("ij,scj->sci", mask_full, values, precision=highest)

    beside = inside_sum(voltage) + halo(voltage)
    bits = sum_bits("region")
    for newton in range(NEWTON):
        last = newton + 1 == NEWTON
        magnitude = voltage[:, 0:1] ** 2 + voltage[:, 1:2] ** 2
        residual = (
            diag_admit * voltage
            - rotate(conductance, susceptance, beside, 1)
            + load_coeff * magnitude * voltage
            - injection
        )
        partial = jnp.sum(residual * residual, axis=(1, 2))
        if bits is None:
            partial = lax.psum(partial, "region")
            chunks = [[]] * SWEEPS
        else:
            chunks = split_even(bits, SWEEPS - 1 if last else SWEEPS)
        update = jnp.zeros_like(voltage)
        for sweep_number in range(SWEEPS):
            forcing = -residual
            if sweep_number > 0:
                partial = sum_rounds(partial, "region", chunks[sweep_number - 1])
                arrived = halo(update)
                partial, arrived = lax.optimization_barrier((partial, arrived))
                forcing = forcing + rotate(conductance, susceptance, arrived, 1)
            forcing = forcing.reshape(scenarios, 2 * buses).astype(jnp.bfloat16)
            update = jnp.dot(forcing, region_inverse, preferred_element_type=jnp.float32).reshape(
                scenarios, 2, buses
            )
        if not last:
            partial = sum_rounds(partial, "region", chunks[SWEEPS - 1])
            extra = inside_sum(update) + halo(update)
            partial, extra = lax.optimization_barrier((partial, extra))
        squares = partial
        damping = jnp.minimum(1.0, trust_radius / jnp.sqrt(squares / (2 * bus_total) + 1e-06))
        step = damping[:, None, None]
        voltage = voltage + step * update
        if not last:
            beside = beside + step * extra
    return voltage


def solution(mesh):
    in_specs = (
        P(None, "region", None),
        P("region", None),
        P("region", None),
        P("region", None),
        P("region"),
        P(),
        P(),
        P(),
        P(),
        P(None, None, "region"),
        P(),
        P("region"),
        P("region"),
        P("region"),
        P("region"),
        P("region", None),
    )
    out_specs = P(None, None, "region")
    return jax.shard_map(local, mesh=mesh, in_specs=in_specs, out_specs=out_specs, check_vma=False)
```

```python
import jax
import jax.numpy as jnp
from jax import lax
from jax.sharding import PartitionSpec as P

RW = 16
NEWTON = 2
SWEEPS = 3


trust_radius = 8.0
highest = lax.Precision.HIGHEST


def from_behind(value, axis, steps):
    count = lax.axis_size(axis)
    first, last = (max(0, -steps), min(count, count - steps))
    return lax.ppermute(value, axis, [(source, source + steps) for source in range(first, last)])


def sum_bits(axis):
    count = lax.axis_size(axis)
    if count & (count - 1):
        return None
    return [1 << b for b in range(count.bit_length() - 1)]


def sum_rounds(value, axis, bits):
    count = lax.axis_size(axis)
    for bit in bits:
        value = value + lax.ppermute(value, axis, [(i, i ^ bit) for i in range(count)])
    return value


def split_even(items, parts):
    cuts = [len(items) * p // parts for p in range(parts + 1)]
    return [items[cuts[p] : cuts[p + 1]] for p in range(parts)]


def rotate(conduct, suscept, beside, axis):
    real_part = jnp.take(beside, 0, axis=axis)
    imag_part = jnp.take(beside, 1, axis=axis)
    return jnp.stack(
        [conduct * real_part - suscept * imag_part, suscept * real_part + conduct * imag_part],
        axis=axis,
    )


def local(
    features,
    line_mask,
    send_rows,
    attach_rows,
    tile_count,
    self_weight,
    neigh_weight,
    layer_bias,
    readout,
    load_table,
    scenario_profile,
    diag_admit,
    conductance,
    susceptance,
    load_coeff,
    region_inverse,
):
    scenarios, buses, width = features.shape
    neighbours, tile_size = send_rows.shape
    offsets = (1, -1, RW, -RW)
    bus_iota = lax.broadcasted_iota(jnp.int32, (neighbours, tile_size, buses), 2)
    live = lax.broadcasted_iota(jnp.int32, (neighbours, tile_size), 1) < tile_count[:, None]
    pick = (send_rows[:, :, None] == bus_iota) & live[:, :, None]
    place = attach_rows[:, :, None] == bus_iota
    pick_half, pick_full = pick.astype(jnp.bfloat16), pick.astype(jnp.float32)
    place_half, place_full = place.astype(jnp.bfloat16), place.astype(jnp.float32)
    mask_half = line_mask.astype(jnp.bfloat16)
    mask_full = line_mask.astype(jnp.float32)

    def exchange(tiles):
        return jnp.stack(
            [from_behind(tiles[k], "region", offsets[k]) for k in range(neighbours)]
        )

    hidden = features
    for number in range(self_weight.shape[0]):
        tiles = jnp.einsum(
            "ktb,sbh->ksth", pick_half, hidden, preferred_element_type=jnp.float32
        ).astype(jnp.bfloat16)
        incoming = exchange(tiles)
        inside = jnp.einsum("ij,sjh->sih", mask_half, hidden, preferred_element_type=jnp.float32)
        own = jnp.einsum(
            "sbh,hk->sbk", hidden, self_weight[number], preferred_element_type=jnp.float32
        )
        border = jnp.einsum(
            "ktb,ksth->sbh", place_half, incoming, preferred_element_type=jnp.float32
        )
        gathered = (0.25 * (inside + border)).astype(jnp.bfloat16)
        summed = (
            own
            + jnp.einsum(
                "sbh,hk->sbk", gathered, neigh_weight[number], preferred_element_type=jnp.float32
            )
            + layer_bias[number]
        )
        hidden = (hidden.astype(jnp.float32) + jax.nn.silu(summed)).astype(jnp.bfloat16)
    flat_start = jnp.array([1.0, 0.0], dtype=jnp.float32)[None, :, None]
    voltage = (
        jnp.einsum("sbh,ch->scb", hidden, readout, preferred_element_type=jnp.float32) + flat_start
    )
    choose = (
        scenario_profile[:, None]
        == lax.broadcasted_iota(jnp.int32, (scenarios, load_table.shape[0]), 1)
    ).astype(jnp.float32)
    injection = jnp.einsum("sp,pcb->scb", choose, load_table, precision=highest)
    bus_total = buses * lax.axis_size("region")

    def halo(values):
        shape = values.shape
        flat = values.reshape((-1,) + shape[-2:])
        tiles = jnp.einsum("ktb,ncb->knct", pick_full, flat, precision=highest)
        incoming = exchange(tiles)
        spread = jnp.einsum("knct,ktb->ncb", incoming, place_full, precision=highest)
        return spread.reshape(shape)

    def inside_sum(values):
        return jnp.einsum("ij,...cj->...ci", mask_full, values, precision=highest)

    def damp(squares):
        return jnp.minimum(1.0, trust_radius / jnp.sqrt(squares / (2 * bus_total) + 1e-06))

    def sweeps(residuals, partial, chunks):
        count = residuals.shape[0]
        update = None
        for sweep_number in range(SWEEPS):
            forcing = -residuals
            if sweep_number > 0:
                arrived = halo(update)
                if chunks:
                    partial = sum_rounds(partial, "region", chunks[sweep_number - 1])
                    partial, arrived = lax.optimization_barrier((partial, arrived))
                forcing = forcing + rotate(conductance, susceptance, arrived, -2)
            forcing = forcing.reshape(count * scenarios, 2 * buses).astype(jnp.bfloat16)
            update = jnp.dot(forcing, region_inverse, preferred_element_type=jnp.float32)
            update = update.reshape(count, scenarios, 2, buses)
        return update, partial

    assert NEWTON == 2
    bits = sum_bits("region")
    beside = inside_sum(voltage) + halo(voltage)
    magnitude = voltage[:, 0:1] ** 2 + voltage[:, 1:2] ** 2
    residual = (
        diag_admit * voltage
        - rotate(conductance, susceptance, beside, 1)
        + load_coeff * magnitude * voltage
        - injection
    )
    partial = jnp.sum(residual * residual, axis=(1, 2))[None]
    update, partial = sweeps(residual[None], partial, None)
    update = update[0]
    extra = inside_sum(update) + halo(update)
    cross = 2.0 * (voltage[:, 0:1] * update[:, 0:1] + voltage[:, 1:2] * update[:, 1:2])
    square = update[:, 0:1] ** 2 + update[:, 1:2] ** 2
    coeffs = jnp.stack(
        [
            residual,
            diag_admit * update
            - rotate(conductance, susceptance, extra, 1)
            + load_coeff * (magnitude * update + cross * voltage),
            load_coeff * (cross * update + square * voltage),
            load_coeff * square * update,
        ]
    )
    terms = coeffs.shape[0]
    powers = [0.0] * (2 * terms - 1)
    for i in range(terms):
        for j in range(i, terms):
            product = jnp.sum(coeffs[i] * coeffs[j], axis=(1, 2))
            powers[i + j] = powers[i + j] + (product if i == j else 2.0 * product)
    partial = jnp.concatenate([partial, jnp.stack(powers)])
    chunks = None if bits is None else split_even(bits, SWEEPS - 1)
    second, partial = sweeps(coeffs, partial, chunks)
    if bits is None:
        partial = lax.psum(partial, "region")
    first_damping = damp(partial[0])
    poly = partial[-1]
    for k in range(len(powers) - 2, -1, -1):
        poly = poly * first_damping + partial[1 + k]
    second_damping = damp(jnp.maximum(poly, 0.0))
    voltage = voltage + first_damping[:, None, None] * update
    step_update = second[-1]
    for k in range(terms - 2, -1, -1):
        step_update = step_update * first_damping[:, None, None] + second[k]
    voltage = voltage + second_damping[:, None, None] * step_update
    return voltage


def solution(mesh):
    in_specs = (
        P(None, "region", None),
        P("region", None),
        P("region", None),
        P("region", None),
        P("region"),
        P(),
        P(),
        P(),
        P(),
        P(None, None, "region"),
        P(),
        P("region"),
        P("region"),
        P("region"),
        P("region"),
        P("region", None),
    )
    out_specs = P(None, None, "region")
    return jax.shard_map(local, mesh=mesh, in_specs=in_specs, out_specs=out_specs, check_vma=False)
```

```python
import jax
import jax.numpy as jnp
from jax import lax
from jax.sharding import PartitionSpec as P

RW = 16
NEWTON = 2
SWEEPS = 3


trust_radius = 8.0
highest = lax.Precision.HIGHEST


def swap_pairs(count, offset, phase):
    pairs = []
    for low in range(count - offset):
        if (low // offset) % 2 == phase:
            pairs += [(low, low + offset), (low + offset, low)]
    return pairs


def sum_bits(axis):
    count = lax.axis_size(axis)
    if count & (count - 1):
        return None
    return [1 << b for b in range(count.bit_length() - 1)]


def sum_rounds(value, axis, bits):
    count = lax.axis_size(axis)
    for bit in bits:
        value = value + lax.ppermute(value, axis, [(i, i ^ bit) for i in range(count)])
    return value


def split_even(items, parts):
    cuts = [len(items) * p // parts for p in range(parts + 1)]
    return [items[cuts[p] : cuts[p + 1]] for p in range(parts)]


def rotate(conduct, suscept, beside, axis):
    real_part = jnp.take(beside, 0, axis=axis)
    imag_part = jnp.take(beside, 1, axis=axis)
    return jnp.stack(
        [conduct * real_part - suscept * imag_part, suscept * real_part + conduct * imag_part],
        axis=axis,
    )


def local(
    features,
    line_mask,
    send_rows,
    attach_rows,
    tile_count,
    self_weight,
    neigh_weight,
    layer_bias,
    readout,
    load_table,
    scenario_profile,
    diag_admit,
    conductance,
    susceptance,
    load_coeff,
    region_inverse,
):
    scenarios, buses, width = features.shape
    neighbours, tile_size = send_rows.shape
    offsets = (1, -1, RW, -RW)
    count = lax.axis_size("region")
    me = lax.axis_index("region")
    routes, send_slots, recv_slots = [], [], []
    for offset, up, down in ((offsets[0], 0, 1), (offsets[2], 2, 3)):
        lower = (me // offset) % 2 == 0
        for phase in (0, 1):
            first = lower if phase == 0 else jnp.logical_not(lower)
            routes.append(swap_pairs(count, offset, phase))
            send_slots.append(jnp.where(first, up, down))
            recv_slots.append(jnp.where(first, down, up))
    send_slots = jnp.stack(send_slots)
    recv_slots = jnp.stack(recv_slots)
    bus_iota = lax.broadcasted_iota(jnp.int32, (neighbours, tile_size, buses), 2)
    live = lax.broadcasted_iota(jnp.int32, (neighbours, tile_size), 1) < tile_count[:, None]
    send_route = jnp.take(send_rows, send_slots, axis=0)
    live_route = jnp.take(live, send_slots, axis=0)
    attach_route = jnp.take(attach_rows, recv_slots, axis=0)
    pick = (send_route[:, :, None] == bus_iota) & live_route[:, :, None]
    place = attach_route[:, :, None] == bus_iota
    pick_half, pick_full = pick.astype(jnp.bfloat16), pick.astype(jnp.float32)
    place_half, place_full = place.astype(jnp.bfloat16), place.astype(jnp.float32)
    mask_half = line_mask.astype(jnp.bfloat16)
    mask_full = line_mask.astype(jnp.float32)

    def exchange(tiles):
        return jnp.stack(
            [lax.ppermute(tiles[j], "region", routes[j]) for j in range(len(routes))]
        )

    hidden = features
    for number in range(self_weight.shape[0]):
        tiles = jnp.einsum(
            "ktb,sbh->ksth", pick_half, hidden, preferred_element_type=jnp.float32
        ).astype(jnp.bfloat16)
        incoming = exchange(tiles)
        inside = jnp.einsum("ij,sjh->sih", mask_half, hidden, preferred_element_type=jnp.float32)
        own = jnp.einsum(
            "sbh,hk->sbk", hidden, self_weight[number], preferred_element_type=jnp.float32
        )
        border = jnp.einsum(
            "ktb,ksth->sbh", place_half, incoming, preferred_element_type=jnp.float32
        )
        gathered = (0.25 * (inside + border)).astype(jnp.bfloat16)
        summed = (
            own
            + jnp.einsum(
                "sbh,hk->sbk", gathered, neigh_weight[number], preferred_element_type=jnp.float32
            )
            + layer_bias[number]
        )
        hidden = (hidden.astype(jnp.float32) + jax.nn.silu(summed)).astype(jnp.bfloat16)
    flat_start = jnp.array([1.0, 0.0], dtype=jnp.float32)[None, :, None]
    voltage = (
        jnp.einsum("sbh,ch->scb", hidden, readout, preferred_element_type=jnp.float32) + flat_start
    )
    choose = (
        scenario_profile[:, None]
        == lax.broadcasted_iota(jnp.int32, (scenarios, load_table.shape[0]), 1)
    ).astype(jnp.float32)
    injection = jnp.einsum("sp,pcb->scb", choose, load_table, precision=highest)
    bus_total = buses * lax.axis_size("region")

    def halo(values):
        shape = values.shape
        flat = values.reshape((-1,) + shape[-2:])
        tiles = jnp.einsum("ktb,ncb->knct", pick_full, flat, precision=highest)
        incoming = exchange(tiles)
        spread = jnp.einsum("knct,ktb->ncb", incoming, place_full, precision=highest)
        return spread.reshape(shape)

    def inside_sum(values):
        return jnp.einsum("ij,...cj->...ci", mask_full, values, precision=highest)

    def damp(squares):
        return jnp.minimum(1.0, trust_radius / jnp.sqrt(squares / (2 * bus_total) + 1e-06))

    def sweeps(residuals, partial, chunks):
        count = residuals.shape[0]
        update = None
        for sweep_number in range(SWEEPS):
            forcing = -residuals
            if sweep_number > 0:
                arrived = halo(update)
                if chunks:
                    partial = sum_rounds(partial, "region", chunks[sweep_number - 1])
                    partial, arrived = lax.optimization_barrier((partial, arrived))
                forcing = forcing + rotate(conductance, susceptance, arrived, -2)
            forcing = forcing.reshape(count * scenarios, 2 * buses).astype(jnp.bfloat16)
            update = jnp.dot(forcing, region_inverse, preferred_element_type=jnp.float32)
            update = update.reshape(count, scenarios, 2, buses)
        return update, partial

    assert NEWTON == 2
    bits = sum_bits("region")
    beside = inside_sum(voltage) + halo(voltage)
    magnitude = voltage[:, 0:1] ** 2 + voltage[:, 1:2] ** 2
    residual = (
        diag_admit * voltage
        - rotate(conductance, susceptance, beside, 1)
        + load_coeff * magnitude * voltage
        - injection
    )
    partial = jnp.sum(residual * residual, axis=(1, 2))[None]
    update, partial = sweeps(residual[None], partial, None)
    update = update[0]
    extra = inside_sum(update) + halo(update)
    cross = 2.0 * (voltage[:, 0:1] * update[:, 0:1] + voltage[:, 1:2] * update[:, 1:2])
    square = update[:, 0:1] ** 2 + update[:, 1:2] ** 2
    coeffs = jnp.stack(
        [
            residual,
            diag_admit * update
            - rotate(conductance, susceptance, extra, 1)
            + load_coeff * (magnitude * update + cross * voltage),
            load_coeff * (cross * update + square * voltage),
            load_coeff * square * update,
        ]
    )
    terms = coeffs.shape[0]
    powers = [0.0] * (2 * terms - 1)
    for i in range(terms):
        for j in range(i, terms):
            product = jnp.sum(coeffs[i] * coeffs[j], axis=(1, 2))
            powers[i + j] = powers[i + j] + (product if i == j else 2.0 * product)
    partial = jnp.concatenate([partial, jnp.stack(powers)])
    chunks = None if bits is None else split_even(bits, SWEEPS - 1)
    second, partial = sweeps(coeffs, partial, chunks)
    if bits is None:
        partial = lax.psum(partial, "region")
    first_damping = damp(partial[0])
    poly = partial[-1]
    for k in range(len(powers) - 2, -1, -1):
        poly = poly * first_damping + partial[1 + k]
    second_damping = damp(jnp.maximum(poly, 0.0))
    voltage = voltage + first_damping[:, None, None] * update
    step_update = second[-1]
    for k in range(terms - 2, -1, -1):
        step_update = step_update * first_damping[:, None, None] + second[k]
    voltage = voltage + second_damping[:, None, None] * step_update
    return voltage


def solution(mesh):
    in_specs = (
        P(None, "region", None),
        P("region", None),
        P("region", None),
        P("region", None),
        P("region"),
        P(),
        P(),
        P(),
        P(),
        P(None, None, "region"),
        P(),
        P("region"),
        P("region"),
        P("region"),
        P("region"),
        P("region", None),
    )
    out_specs = P(None, None, "region")
    return jax.shard_map(local, mesh=mesh, in_specs=in_specs, out_specs=out_specs, check_vma=False)
```

```python
import jax
import jax.numpy as jnp
from jax import lax
from jax.sharding import PartitionSpec as P

RW = 16
NEWTON = 2
SWEEPS = 3


trust_radius = 8.0
highest = lax.Precision.HIGHEST


def swap_pairs(count, offset, phase):
    pairs = []
    for low in range(count - offset):
        if (low // offset) % 2 == phase:
            pairs += [(low, low + offset), (low + offset, low)]
    return pairs


def sum_bits(axis):
    count = lax.axis_size(axis)
    if count & (count - 1):
        return None
    return [1 << b for b in range(count.bit_length() - 1)]


def sum_rounds(value, axis, bits):
    count = lax.axis_size(axis)
    for bit in bits:
        value = value + lax.ppermute(value, axis, [(i, i ^ bit) for i in range(count)])
    return value


def split_even(items, parts):
    cuts = [len(items) * p // parts for p in range(parts + 1)]
    return [items[cuts[p] : cuts[p + 1]] for p in range(parts)]


def rotate(conduct, suscept, beside, axis):
    real_part = jnp.take(beside, 0, axis=axis)
    imag_part = jnp.take(beside, 1, axis=axis)
    return jnp.stack(
        [conduct * real_part - suscept * imag_part, suscept * real_part + conduct * imag_part],
        axis=axis,
    )


def local(
    features,
    line_mask,
    send_rows,
    attach_rows,
    tile_count,
    self_weight,
    neigh_weight,
    layer_bias,
    readout,
    load_table,
    scenario_profile,
    diag_admit,
    conductance,
    susceptance,
    load_coeff,
    region_inverse,
):
    scenarios, buses, width = features.shape
    neighbours, tile_size = send_rows.shape
    offsets = (1, -1, RW, -RW)
    count = lax.axis_size("region")
    me = lax.axis_index("region")
    routes, send_slots, recv_slots = [], [], []
    for offset, up, down in ((offsets[0], 0, 1), (offsets[2], 2, 3)):
        lower = (me // offset) % 2 == 0
        for phase in (0, 1):
            first = lower if phase == 0 else jnp.logical_not(lower)
            routes.append(swap_pairs(count, offset, phase))
            send_slots.append(jnp.where(first, up, down))
            recv_slots.append(jnp.where(first, down, up))
    send_slots = jnp.stack(send_slots)
    recv_slots = jnp.stack(recv_slots)
    bus_iota = lax.broadcasted_iota(jnp.int32, (neighbours, tile_size, buses), 2)
    live = lax.broadcasted_iota(jnp.int32, (neighbours, tile_size), 1) < tile_count[:, None]
    send_route = jnp.take(send_rows, send_slots, axis=0)
    live_route = jnp.take(live, send_slots, axis=0)
    attach_route = jnp.take(attach_rows, recv_slots, axis=0)
    pick = (send_route[:, :, None] == bus_iota) & live_route[:, :, None]
    place = attach_route[:, :, None] == bus_iota
    pick_half, pick_full = pick.astype(jnp.bfloat16), pick.astype(jnp.float32)
    place_half, place_full = place.astype(jnp.bfloat16), place.astype(jnp.float32)
    mask_half = line_mask.astype(jnp.bfloat16)
    mask_full = line_mask.astype(jnp.float32)

    def exchange(tiles):
        return jnp.stack(
            [lax.ppermute(tiles[j], "region", routes[j]) for j in range(len(routes))]
        )

    readout_pad = jnp.pad(readout.T, ((0, 0), (0, 128 - readout.shape[0])))
    flat_start = jnp.array([1.0, 0.0], dtype=jnp.float32)[None, :, None]

    def layer(hidden, incoming, number):
        inside = jnp.einsum("ij,sjh->sih", mask_half, hidden, preferred_element_type=jnp.float32)
        own = jnp.einsum(
            "sbh,hk->sbk", hidden, self_weight[number], preferred_element_type=jnp.float32
        )
        border = jnp.einsum(
            "ktb,ksth->sbh", place_half, incoming, preferred_element_type=jnp.float32
        )
        gathered = (0.25 * (inside + border)).astype(jnp.bfloat16)
        summed = (
            own
            + jnp.einsum(
                "sbh,hk->sbk", gathered, neigh_weight[number], preferred_element_type=jnp.float32
            )
            + layer_bias[number]
        )
        return (hidden.astype(jnp.float32) + jax.nn.silu(summed)).astype(jnp.bfloat16)

    def tiles_of(hidden):
        return jnp.einsum(
            "ktb,sbh->ksth", pick_half, hidden, preferred_element_type=jnp.float32
        ).astype(jnp.bfloat16)

    groups = 2 if scenarios % 2 == 0 else 1
    part = scenarios // groups
    parts = [features[g * part : (g + 1) * part] for g in range(groups)]
    for number in range(self_weight.shape[0]):
        arrived = [exchange(tiles_of(hidden)) for hidden in parts]
        parts = [layer(hidden, got, number) for hidden, got in zip(parts, arrived)]
    starts = []
    for hidden in parts:
        projected = jnp.dot(
            hidden.reshape(-1, width), readout_pad, preferred_element_type=jnp.float32
        )[:, : readout.shape[0]]
        starts.append(jnp.transpose(projected.reshape(part, buses, -1), (0, 2, 1)))
    voltage = jnp.concatenate(starts) + flat_start
    choose = (
        scenario_profile[:, None]
        == lax.broadcasted_iota(jnp.int32, (scenarios, load_table.shape[0]), 1)
    ).astype(jnp.float32)
    injection = jnp.einsum("sp,pcb->scb", choose, load_table, precision=highest)
    bus_total = buses * lax.axis_size("region")

    def halo(values):
        shape = values.shape
        flat = values.reshape((-1,) + shape[-2:])
        tiles = jnp.einsum("ktb,ncb->knct", pick_full, flat, precision=highest)
        incoming = exchange(tiles)
        spread = jnp.einsum("knct,ktb->ncb", incoming, place_full, precision=highest)
        return spread.reshape(shape)

    def inside_sum(values):
        return jnp.einsum("ij,...cj->...ci", mask_full, values, precision=highest)

    def damp(squares):
        return jnp.minimum(1.0, trust_radius / jnp.sqrt(squares / (2 * bus_total) + 1e-06))

    def sweeps(residuals, partial, chunks):
        count = residuals.shape[0]
        update = None
        for sweep_number in range(SWEEPS):
            forcing = -residuals
            if sweep_number > 0:
                arrived = halo(update)
                if chunks:
                    partial = sum_rounds(partial, "region", chunks[sweep_number - 1])
                    partial, arrived = lax.optimization_barrier((partial, arrived))
                forcing = forcing + rotate(conductance, susceptance, arrived, -2)
            forcing = forcing.reshape(count * scenarios, 2 * buses).astype(jnp.bfloat16)
            update = jnp.dot(forcing, region_inverse, preferred_element_type=jnp.float32)
            update = update.reshape(count, scenarios, 2, buses)
        return update, partial

    assert NEWTON == 2
    bits = sum_bits("region")
    beside = inside_sum(voltage) + halo(voltage)
    magnitude = voltage[:, 0:1] ** 2 + voltage[:, 1:2] ** 2
    residual = (
        diag_admit * voltage
        - rotate(conductance, susceptance, beside, 1)
        + load_coeff * magnitude * voltage
        - injection
    )
    partial = jnp.sum(residual * residual, axis=(1, 2))[None]
    update, partial = sweeps(residual[None], partial, None)
    update = update[0]
    extra = inside_sum(update) + halo(update)
    cross = 2.0 * (voltage[:, 0:1] * update[:, 0:1] + voltage[:, 1:2] * update[:, 1:2])
    square = update[:, 0:1] ** 2 + update[:, 1:2] ** 2
    coeffs = jnp.stack(
        [
            residual,
            diag_admit * update
            - rotate(conductance, susceptance, extra, 1)
            + load_coeff * (magnitude * update + cross * voltage),
            load_coeff * (cross * update + square * voltage),
            load_coeff * square * update,
        ]
    )
    terms = coeffs.shape[0]
    powers = [0.0] * (2 * terms - 1)
    for i in range(terms):
        for j in range(i, terms):
            product = jnp.sum(coeffs[i] * coeffs[j], axis=(1, 2))
            powers[i + j] = powers[i + j] + (product if i == j else 2.0 * product)
    partial = jnp.concatenate([partial, jnp.stack(powers)])
    chunks = None if bits is None else split_even(bits, SWEEPS - 1)
    second, partial = sweeps(coeffs, partial, chunks)
    if bits is None:
        partial = lax.psum(partial, "region")
    first_damping = damp(partial[0])
    poly = partial[-1]
    for k in range(len(powers) - 2, -1, -1):
        poly = poly * first_damping + partial[1 + k]
    second_damping = damp(jnp.maximum(poly, 0.0))
    voltage = voltage + first_damping[:, None, None] * update
    step_update = second[-1]
    for k in range(terms - 2, -1, -1):
        step_update = step_update * first_damping[:, None, None] + second[k]
    voltage = voltage + second_damping[:, None, None] * step_update
    return voltage


def solution(mesh):
    in_specs = (
        P(None, "region", None),
        P("region", None),
        P("region", None),
        P("region", None),
        P("region"),
        P(),
        P(),
        P(),
        P(),
        P(None, None, "region"),
        P(),
        P("region"),
        P("region"),
        P("region"),
        P("region"),
        P("region", None),
    )
    out_specs = P(None, None, "region")
    return jax.shard_map(local, mesh=mesh, in_specs=in_specs, out_specs=out_specs, check_vma=False)
```

```python
import jax
import jax.numpy as jnp
from jax import lax
from jax.sharding import PartitionSpec as P

RW = 16
NEWTON = 2
SWEEPS = 3


trust_radius = 8.0
highest = lax.Precision.HIGHEST


def swap_pairs(count, offset, phase):
    pairs = []
    for low in range(count - offset):
        if (low // offset) % 2 == phase:
            pairs += [(low, low + offset), (low + offset, low)]
    return pairs


def sum_bits(axis):
    count = lax.axis_size(axis)
    if count & (count - 1):
        return None
    return [1 << b for b in range(count.bit_length() - 1)]


def sum_rounds(value, axis, bits):
    count = lax.axis_size(axis)
    for bit in bits:
        value = value + lax.ppermute(value, axis, [(i, i ^ bit) for i in range(count)])
    return value


def split_even(items, parts):
    cuts = [len(items) * p // parts for p in range(parts + 1)]
    return [items[cuts[p] : cuts[p + 1]] for p in range(parts)]


def rotate(conduct, suscept, beside, axis):
    real_part = jnp.take(beside, 0, axis=axis)
    imag_part = jnp.take(beside, 1, axis=axis)
    return jnp.stack(
        [conduct * real_part - suscept * imag_part, suscept * real_part + conduct * imag_part],
        axis=axis,
    )


def local(
    features,
    line_mask,
    send_rows,
    attach_rows,
    tile_count,
    self_weight,
    neigh_weight,
    layer_bias,
    readout,
    load_table,
    scenario_profile,
    diag_admit,
    conductance,
    susceptance,
    load_coeff,
    region_inverse,
):
    scenarios, buses, width = features.shape
    neighbours, tile_size = send_rows.shape
    offsets = (1, -1, RW, -RW)
    count = lax.axis_size("region")
    me = lax.axis_index("region")
    routes, send_slots, recv_slots = [], [], []
    for offset, up, down in ((offsets[0], 0, 1), (offsets[2], 2, 3)):
        lower = (me // offset) % 2 == 0
        for phase in (0, 1):
            first = lower if phase == 0 else jnp.logical_not(lower)
            routes.append(swap_pairs(count, offset, phase))
            send_slots.append(jnp.where(first, up, down))
            recv_slots.append(jnp.where(first, down, up))
    send_slots = jnp.stack(send_slots)
    recv_slots = jnp.stack(recv_slots)
    bus_iota = lax.broadcasted_iota(jnp.int32, (neighbours, tile_size, buses), 2)
    live = lax.broadcasted_iota(jnp.int32, (neighbours, tile_size), 1) < tile_count[:, None]
    send_route = jnp.take(send_rows, send_slots, axis=0)
    live_route = jnp.take(live, send_slots, axis=0)
    attach_route = jnp.take(attach_rows, recv_slots, axis=0)
    pick = (send_route[:, :, None] == bus_iota) & live_route[:, :, None]
    place = attach_route[:, :, None] == bus_iota
    pick_half, pick_full = pick.astype(jnp.bfloat16), pick.astype(jnp.float32)
    place_half, place_full = place.astype(jnp.bfloat16), place.astype(jnp.float32)
    mask_half = line_mask.astype(jnp.bfloat16)
    mask_full = line_mask.astype(jnp.float32)

    def exchange(tiles):
        return jnp.stack(
            [lax.ppermute(tiles[j], "region", routes[j]) for j in range(len(routes))]
        )

    hidden = features
    for number in range(self_weight.shape[0]):
        tiles = jnp.einsum(
            "ktb,sbh->ksth", pick_half, hidden, preferred_element_type=jnp.float32
        ).astype(jnp.bfloat16)
        incoming = exchange(tiles)
        inside = jnp.einsum("ij,sjh->sih", mask_half, hidden, preferred_element_type=jnp.float32)
        own = jnp.einsum(
            "sbh,hk->sbk", hidden, self_weight[number], preferred_element_type=jnp.float32
        )
        border = jnp.einsum(
            "ktb,ksth->sbh", place_half, incoming, preferred_element_type=jnp.float32
        )
        gathered = (0.25 * (inside + border)).astype(jnp.bfloat16)
        summed = (
            own
            + jnp.einsum(
                "sbh,hk->sbk", gathered, neigh_weight[number], preferred_element_type=jnp.float32
            )
            + layer_bias[number]
        )
        hidden = (hidden.astype(jnp.float32) + jax.nn.silu(summed)).astype(jnp.bfloat16)
    flat_start = jnp.array([1.0, 0.0], dtype=jnp.float32)[None, :, None]
    readout_pad = jnp.pad(readout.T, ((0, 0), (0, 128 - readout.shape[0])))
    projected = jnp.dot(hidden.reshape(-1, width), readout_pad, preferred_element_type=jnp.float32)
    projected = projected[:, : readout.shape[0]].reshape(scenarios, buses, -1)
    voltage = jnp.transpose(projected, (0, 2, 1)) + flat_start
    choose = (
        scenario_profile[:, None]
        == lax.broadcasted_iota(jnp.int32, (scenarios, load_table.shape[0]), 1)
    ).astype(jnp.float32)
    injection = jnp.einsum("sp,pcb->scb", choose, load_table, precision=highest)
    bus_total = buses * lax.axis_size("region")

    def halo(values):
        shape = values.shape
        flat = values.reshape((-1,) + shape[-2:])
        tiles = jnp.einsum("ktb,ncb->knct", pick_full, flat, precision=highest)
        incoming = exchange(tiles)
        spread = jnp.einsum("knct,ktb->ncb", incoming, place_full, precision=highest)
        return spread.reshape(shape)

    def inside_sum(values):
        return jnp.einsum("ij,...cj->...ci", mask_full, values, precision=highest)

    def damp(squares):
        return jnp.minimum(1.0, trust_radius / jnp.sqrt(squares / (2 * bus_total) + 1e-06))

    def sweeps(residuals, partial, chunks):
        count = residuals.shape[0]
        update = None
        for sweep_number in range(SWEEPS):
            forcing = -residuals
            if sweep_number > 0:
                arrived = halo(update)
                if chunks:
                    partial = sum_rounds(partial, "region", chunks[sweep_number - 1])
                    partial, arrived = lax.optimization_barrier((partial, arrived))
                forcing = forcing + rotate(conductance, susceptance, arrived, -2)
            forcing = forcing.reshape(count * scenarios, 2 * buses).astype(jnp.bfloat16)
            update = jnp.dot(forcing, region_inverse, preferred_element_type=jnp.float32)
            update = update.reshape(count, scenarios, 2, buses)
        return update, partial

    assert NEWTON == 2
    bits = sum_bits("region")
    beside = inside_sum(voltage) + halo(voltage)
    magnitude = voltage[:, 0:1] ** 2 + voltage[:, 1:2] ** 2
    residual = (
        diag_admit * voltage
        - rotate(conductance, susceptance, beside, 1)
        + load_coeff * magnitude * voltage
        - injection
    )
    partial = jnp.sum(residual * residual, axis=(1, 2))[None]
    update, partial = sweeps(residual[None], partial, None)
    update = update[0]
    extra = inside_sum(update) + halo(update)
    cross = 2.0 * (voltage[:, 0:1] * update[:, 0:1] + voltage[:, 1:2] * update[:, 1:2])
    square = update[:, 0:1] ** 2 + update[:, 1:2] ** 2
    coeffs = jnp.stack(
        [
            residual,
            diag_admit * update
            - rotate(conductance, susceptance, extra, 1)
            + load_coeff * (magnitude * update + cross * voltage),
            load_coeff * (cross * update + square * voltage),
            load_coeff * square * update,
        ]
    )
    terms = coeffs.shape[0]
    powers = [0.0] * (2 * terms - 1)
    for i in range(terms):
        for j in range(i, terms):
            product = jnp.sum(coeffs[i] * coeffs[j], axis=(1, 2))
            powers[i + j] = powers[i + j] + (product if i == j else 2.0 * product)
    partial = jnp.concatenate([partial, jnp.stack(powers)])
    chunks = None if bits is None else split_even(bits, SWEEPS - 1)
    second, partial = sweeps(coeffs, partial, chunks)
    if bits is None:
        partial = lax.psum(partial, "region")
    first_damping = damp(partial[0])
    poly = partial[-1]
    for k in range(len(powers) - 2, -1, -1):
        poly = poly * first_damping + partial[1 + k]
    second_damping = damp(jnp.maximum(poly, 0.0))
    voltage = voltage + first_damping[:, None, None] * update
    step_update = second[-1]
    for k in range(terms - 2, -1, -1):
        step_update = step_update * first_damping[:, None, None] + second[k]
    voltage = voltage + second_damping[:, None, None] * step_update
    return voltage


def solution(mesh):
    in_specs = (
        P(None, "region", None),
        P("region", None),
        P("region", None),
        P("region", None),
        P("region"),
        P(),
        P(),
        P(),
        P(),
        P(None, None, "region"),
        P(),
        P("region"),
        P("region"),
        P("region"),
        P("region"),
        P("region", None),
    )
    out_specs = P(None, None, "region")
    return jax.shard_map(local, mesh=mesh, in_specs=in_specs, out_specs=out_specs, check_vma=False)
```

```python
import jax
import jax.numpy as jnp
from jax import lax
from jax.sharding import PartitionSpec as P

RW = 16
NEWTON = 2
SWEEPS = 3


trust_radius = 8.0
highest = lax.Precision.HIGHEST


def swap_pairs(count, offset, phase):
    pairs = []
    for low in range(count - offset):
        if (low // offset) % 2 == phase:
            pairs += [(low, low + offset), (low + offset, low)]
    return pairs


RINGS = (8, 4, 4, 2)


def sum_bits(axis):
    count = lax.axis_size(axis)
    if count & (count - 1):
        return None
    sizes = RINGS
    total = 1
    for size in sizes:
        total *= size
    if total != count:
        return [1 << b for b in range(count.bit_length() - 1)]
    near = {2: [1], 4: [1, 3], 8: [1, 2, 7]}
    masks, stride = [], 1
    for size in reversed(sizes):
        masks += [m * stride for m in near[size]]
        stride *= size
    return masks


def sum_rounds(value, axis, bits):
    count = lax.axis_size(axis)
    for bit in bits:
        value = value + lax.ppermute(value, axis, [(i, i ^ bit) for i in range(count)])
    return value


def split_even(items, parts):
    cuts = [len(items) * p // parts for p in range(parts + 1)]
    return [items[cuts[p] : cuts[p + 1]] for p in range(parts)]


def rotate(conduct, suscept, beside, axis):
    real_part = jnp.take(beside, 0, axis=axis)
    imag_part = jnp.take(beside, 1, axis=axis)
    return jnp.stack(
        [conduct * real_part - suscept * imag_part, suscept * real_part + conduct * imag_part],
        axis=axis,
    )


def local(
    features,
    line_mask,
    send_rows,
    attach_rows,
    tile_count,
    self_weight,
    neigh_weight,
    layer_bias,
    readout,
    load_table,
    scenario_profile,
    diag_admit,
    conductance,
    susceptance,
    load_coeff,
    region_inverse,
):
    scenarios, buses, width = features.shape
    neighbours, tile_size = send_rows.shape
    offsets = (1, -1, RW, -RW)
    count = lax.axis_size("region")
    me = lax.axis_index("region")
    routes, send_slots, recv_slots = [], [], []
    for offset, up, down in ((offsets[0], 0, 1), (offsets[2], 2, 3)):
        lower = (me // offset) % 2 == 0
        for phase in (0, 1):
            first = lower if phase == 0 else jnp.logical_not(lower)
            routes.append(swap_pairs(count, offset, phase))
            send_slots.append(jnp.where(first, up, down))
            recv_slots.append(jnp.where(first, down, up))
    send_slots = jnp.stack(send_slots)
    recv_slots = jnp.stack(recv_slots)
    bus_iota = lax.broadcasted_iota(jnp.int32, (neighbours, tile_size, buses), 2)
    live = lax.broadcasted_iota(jnp.int32, (neighbours, tile_size), 1) < tile_count[:, None]
    send_route = jnp.take(send_rows, send_slots, axis=0)
    live_route = jnp.take(live, send_slots, axis=0)
    attach_route = jnp.take(attach_rows, recv_slots, axis=0)
    pick = (send_route[:, :, None] == bus_iota) & live_route[:, :, None]
    place = attach_route[:, :, None] == bus_iota
    pick_half, pick_full = pick.astype(jnp.bfloat16), pick.astype(jnp.float32)
    place_half, place_full = place.astype(jnp.bfloat16), place.astype(jnp.float32)
    mask_half = line_mask.astype(jnp.bfloat16)
    mask_full = line_mask.astype(jnp.float32)

    def exchange(tiles):
        return jnp.stack(
            [lax.ppermute(tiles[j], "region", routes[j]) for j in range(len(routes))]
        )

    hidden = features
    for number in range(self_weight.shape[0]):
        tiles = jnp.einsum(
            "ktb,sbh->ksth", pick_half, hidden, preferred_element_type=jnp.float32
        ).astype(jnp.bfloat16)
        incoming = exchange(tiles)
        inside = jnp.einsum("ij,sjh->sih", mask_half, hidden, preferred_element_type=jnp.float32)
        own = jnp.einsum(
            "sbh,hk->sbk", hidden, self_weight[number], preferred_element_type=jnp.float32
        )
        border = jnp.einsum(
            "ktb,ksth->sbh", place_half, incoming, preferred_element_type=jnp.float32
        )
        gathered = (0.25 * (inside + border)).astype(jnp.bfloat16)
        summed = (
            own
            + jnp.einsum(
                "sbh,hk->sbk", gathered, neigh_weight[number], preferred_element_type=jnp.float32
            )
            + layer_bias[number]
        )
        hidden = (hidden.astype(jnp.float32) + jax.nn.silu(summed)).astype(jnp.bfloat16)
    flat_start = jnp.array([1.0, 0.0], dtype=jnp.float32)[None, :, None]
    voltage = (
        jnp.einsum("sbh,ch->scb", hidden, readout, preferred_element_type=jnp.float32) + flat_start
    )
    choose = (
        scenario_profile[:, None]
        == lax.broadcasted_iota(jnp.int32, (scenarios, load_table.shape[0]), 1)
    ).astype(jnp.float32)
    injection = jnp.einsum("sp,pcb->scb", choose, load_table, precision=highest)
    bus_total = buses * lax.axis_size("region")

    def halo(values):
        shape = values.shape
        flat = values.reshape((-1,) + shape[-2:])
        tiles = jnp.einsum("ktb,ncb->knct", pick_full, flat, precision=highest)
        incoming = exchange(tiles)
        spread = jnp.einsum("knct,ktb->ncb", incoming, place_full, precision=highest)
        return spread.reshape(shape)

    def inside_sum(values):
        return jnp.einsum("ij,...cj->...ci", mask_full, values, precision=highest)

    def damp(squares):
        return jnp.minimum(1.0, trust_radius / jnp.sqrt(squares / (2 * bus_total) + 1e-06))

    def sweeps(residuals, partial, chunks):
        count = residuals.shape[0]
        update = None
        for sweep_number in range(SWEEPS):
            forcing = -residuals
            if sweep_number > 0:
                arrived = halo(update)
                if chunks:
                    partial = sum_rounds(partial, "region", chunks[sweep_number - 1])
                    partial, arrived = lax.optimization_barrier((partial, arrived))
                forcing = forcing + rotate(conductance, susceptance, arrived, -2)
            forcing = forcing.reshape(count * scenarios, 2 * buses).astype(jnp.bfloat16)
            update = jnp.dot(forcing, region_inverse, preferred_element_type=jnp.float32)
            update = update.reshape(count, scenarios, 2, buses)
        return update, partial

    assert NEWTON == 2
    bits = sum_bits("region")
    beside = inside_sum(voltage) + halo(voltage)
    magnitude = voltage[:, 0:1] ** 2 + voltage[:, 1:2] ** 2
    residual = (
        diag_admit * voltage
        - rotate(conductance, susceptance, beside, 1)
        + load_coeff * magnitude * voltage
        - injection
    )
    partial = jnp.sum(residual * residual, axis=(1, 2))[None]
    update, partial = sweeps(residual[None], partial, None)
    update = update[0]
    extra = inside_sum(update) + halo(update)
    cross = 2.0 * (voltage[:, 0:1] * update[:, 0:1] + voltage[:, 1:2] * update[:, 1:2])
    square = update[:, 0:1] ** 2 + update[:, 1:2] ** 2
    coeffs = jnp.stack(
        [
            residual,
            diag_admit * update
            - rotate(conductance, susceptance, extra, 1)
            + load_coeff * (magnitude * update + cross * voltage),
            load_coeff * (cross * update + square * voltage),
            load_coeff * square * update,
        ]
    )
    terms = coeffs.shape[0]
    powers = [0.0] * (2 * terms - 1)
    for i in range(terms):
        for j in range(i, terms):
            product = jnp.sum(coeffs[i] * coeffs[j], axis=(1, 2))
            powers[i + j] = powers[i + j] + (product if i == j else 2.0 * product)
    partial = jnp.concatenate([partial, jnp.stack(powers)])
    chunks = None if bits is None else split_even(bits, SWEEPS - 1)
    second, partial = sweeps(coeffs, partial, chunks)
    if bits is None:
        partial = lax.psum(partial, "region")
    first_damping = damp(partial[0])
    poly = partial[-1]
    for k in range(len(powers) - 2, -1, -1):
        poly = poly * first_damping + partial[1 + k]
    second_damping = damp(jnp.maximum(poly, 0.0))
    voltage = voltage + first_damping[:, None, None] * update
    step_update = second[-1]
    for k in range(terms - 2, -1, -1):
        step_update = step_update * first_damping[:, None, None] + second[k]
    voltage = voltage + second_damping[:, None, None] * step_update
    return voltage


def solution(mesh):
    in_specs = (
        P(None, "region", None),
        P("region", None),
        P("region", None),
        P("region", None),
        P("region"),
        P(),
        P(),
        P(),
        P(),
        P(None, None, "region"),
        P(),
        P("region"),
        P("region"),
        P("region"),
        P("region"),
        P("region", None),
    )
    out_specs = P(None, None, "region")
    return jax.shard_map(local, mesh=mesh, in_specs=in_specs, out_specs=out_specs, check_vma=False)
```

```python
import jax
import jax.numpy as jnp
from jax import lax
from jax.sharding import PartitionSpec as P

RW = 16
NEWTON = 2
SWEEPS = 3


trust_radius = 8.0
highest = lax.Precision.HIGHEST


def swap_pairs(count, offset, phase):
    pairs = []
    for low in range(count - offset):
        if (low // offset) % 2 == phase:
            pairs += [(low, low + offset), (low + offset, low)]
    return pairs


RINGS = (8, 4, 4, 2)


def sum_bits(axis):
    count = lax.axis_size(axis)
    if count & (count - 1):
        return None
    sizes = RINGS
    total = 1
    for size in sizes:
        total *= size
    if total != count:
        return [1 << b for b in range(count.bit_length() - 1)]
    near = {2: [1], 4: [1, 3], 8: [1, 2, 7]}
    masks, stride = [], 1
    for size in reversed(sizes):
        masks += [m * stride for m in near[size]]
        stride *= size
    return masks


def sum_rounds(value, axis, bits):
    count = lax.axis_size(axis)
    for bit in bits:
        value = value + lax.ppermute(value, axis, [(i, i ^ bit) for i in range(count)])
    return value


def split_even(items, parts):
    cuts = [len(items) * p // parts for p in range(parts + 1)]
    return [items[cuts[p] : cuts[p + 1]] for p in range(parts)]


def rotate(conduct, suscept, beside, axis):
    real_part = jnp.take(beside, 0, axis=axis)
    imag_part = jnp.take(beside, 1, axis=axis)
    return jnp.stack(
        [conduct * real_part - suscept * imag_part, suscept * real_part + conduct * imag_part],
        axis=axis,
    )


def local(
    features,
    line_mask,
    send_rows,
    attach_rows,
    tile_count,
    self_weight,
    neigh_weight,
    layer_bias,
    readout,
    load_table,
    scenario_profile,
    diag_admit,
    conductance,
    susceptance,
    load_coeff,
    region_inverse,
):
    scenarios, buses, width = features.shape
    neighbours, tile_size = send_rows.shape
    offsets = (1, -1, RW, -RW)
    count = lax.axis_size("region")
    me = lax.axis_index("region")
    routes, send_slots, recv_slots = [], [], []
    for offset, up, down in ((offsets[0], 0, 1), (offsets[2], 2, 3)):
        lower = (me // offset) % 2 == 0
        for phase in (0, 1):
            first = lower if phase == 0 else jnp.logical_not(lower)
            routes.append(swap_pairs(count, offset, phase))
            send_slots.append(jnp.where(first, up, down))
            recv_slots.append(jnp.where(first, down, up))
    send_slots = jnp.stack(send_slots)
    recv_slots = jnp.stack(recv_slots)
    bus_iota = lax.broadcasted_iota(jnp.int32, (neighbours, tile_size, buses), 2)
    live = lax.broadcasted_iota(jnp.int32, (neighbours, tile_size), 1) < tile_count[:, None]
    send_route = jnp.take(send_rows, send_slots, axis=0)
    live_route = jnp.take(live, send_slots, axis=0)
    attach_route = jnp.take(attach_rows, recv_slots, axis=0)
    pick = (send_route[:, :, None] == bus_iota) & live_route[:, :, None]
    place = attach_route[:, :, None] == bus_iota
    pick_half, pick_full = pick.astype(jnp.bfloat16), pick.astype(jnp.float32)
    place_half, place_full = place.astype(jnp.bfloat16), place.astype(jnp.float32)
    mask_half = line_mask.astype(jnp.bfloat16)
    mask_full = line_mask.astype(jnp.float32)

    def exchange(tiles):
        return jnp.stack(
            [lax.ppermute(tiles[j], "region", routes[j]) for j in range(len(routes))]
        )

    hidden = features
    for number in range(self_weight.shape[0]):
        tiles = jnp.einsum(
            "ktb,sbh->ksth", pick_half, hidden, preferred_element_type=jnp.float32
        ).astype(jnp.bfloat16)
        incoming = exchange(tiles)
        inside = jnp.einsum("ij,sjh->sih", mask_half, hidden, preferred_element_type=jnp.float32)
        own = jnp.einsum(
            "sbh,hk->sbk", hidden, self_weight[number], preferred_element_type=jnp.float32
        )
        border = jnp.einsum(
            "ktb,ksth->sbh", place_half, incoming, preferred_element_type=jnp.float32
        )
        gathered = (0.25 * (inside + border)).astype(jnp.bfloat16)
        summed = (
            own
            + jnp.einsum(
                "sbh,hk->sbk", gathered, neigh_weight[number], preferred_element_type=jnp.float32
            )
            + layer_bias[number]
        )
        hidden = (hidden.astype(jnp.float32) + jax.nn.silu(summed)).astype(jnp.bfloat16)
    flat_start = jnp.array([1.0, 0.0], dtype=jnp.float32)[None, :, None]
    voltage = (
        jnp.einsum("sbh,ch->scb", hidden, readout, preferred_element_type=jnp.float32) + flat_start
    )
    choose = (
        scenario_profile[:, None]
        == lax.broadcasted_iota(jnp.int32, (scenarios, load_table.shape[0]), 1)
    ).astype(jnp.float32)
    injection = jnp.einsum("sp,pcb->scb", choose, load_table, precision=highest)
    bus_total = buses * lax.axis_size("region")

    def halo(values, payload=None):
        shape = values.shape
        flat = values.reshape((-1,) + shape[-2:])
        tiles = jnp.einsum("ktb,ncb->knct", pick_full, flat, precision=highest)
        rows = flat.shape[0]
        if payload is not None:
            cell = tiles.shape[-2] * tiles.shape[-1]
            packed = jnp.pad(payload.reshape(-1), (0, cell - payload.size))
            packed = packed.reshape((1, 1) + tiles.shape[-2:])
            packed = jnp.broadcast_to(packed, (tiles.shape[0], 1) + tiles.shape[-2:])
            tiles = jnp.concatenate([tiles, packed], axis=1)
        incoming = exchange(tiles)
        spread = jnp.einsum(
            "knct,ktb->ncb", incoming[:, :rows], place_full, precision=highest
        ).reshape(shape)
        if payload is None:
            return spread
        carried = incoming[:, rows].reshape(incoming.shape[0], -1)[:, : payload.size]
        return spread, carried.reshape((incoming.shape[0],) + payload.shape)

    def inside_sum(values):
        return jnp.einsum("ij,...cj->...ci", mask_full, values, precision=highest)

    def damp(squares):
        return jnp.minimum(1.0, trust_radius / jnp.sqrt(squares / (2 * bus_total) + 1e-06))

    def sweeps(residuals, partial, plan):
        count = residuals.shape[0]
        update = None
        for sweep_number in range(SWEEPS):
            forcing = -residuals
            if sweep_number > 0:
                carry, masks = plan[sweep_number - 1] if plan else (None, [])
                if carry is None:
                    arrived = halo(update)
                    if masks:
                        partial = sum_rounds(partial, "region", masks)
                        partial, arrived = lax.optimization_barrier((partial, arrived))
                else:
                    arrived, carried = halo(update, partial)
                    partial = sum_rounds(partial + carried[carry], "region", masks)
                forcing = forcing + rotate(conductance, susceptance, arrived, -2)
            forcing = forcing.reshape(count * scenarios, 2 * buses).astype(jnp.bfloat16)
            update = jnp.dot(forcing, region_inverse, preferred_element_type=jnp.float32)
            update = update.reshape(count, scenarios, 2, buses)
        return update, partial

    assert NEWTON == 2
    bits = sum_bits("region")
    beside = inside_sum(voltage) + halo(voltage)
    magnitude = voltage[:, 0:1] ** 2 + voltage[:, 1:2] ** 2
    residual = (
        diag_admit * voltage
        - rotate(conductance, susceptance, beside, 1)
        + load_coeff * magnitude * voltage
        - injection
    )
    partial = jnp.sum(residual * residual, axis=(1, 2))[None]
    update, partial = sweeps(residual[None], partial, None)
    update = update[0]
    extra = inside_sum(update) + halo(update)
    cross = 2.0 * (voltage[:, 0:1] * update[:, 0:1] + voltage[:, 1:2] * update[:, 1:2])
    square = update[:, 0:1] ** 2 + update[:, 1:2] ** 2
    coeffs = jnp.stack(
        [
            residual,
            diag_admit * update
            - rotate(conductance, susceptance, extra, 1)
            + load_coeff * (magnitude * update + cross * voltage),
            load_coeff * (cross * update + square * voltage),
            load_coeff * square * update,
        ]
    )
    terms = coeffs.shape[0]
    powers = [0.0] * (2 * terms - 1)
    for i in range(terms):
        for j in range(i, terms):
            product = jnp.sum(coeffs[i] * coeffs[j], axis=(1, 2))
            powers[i + j] = powers[i + j] + (product if i == j else 2.0 * product)
    partial = jnp.concatenate([partial, jnp.stack(powers)])
    if bits == [1, 2, 6, 8, 24, 32, 64, 224] and SWEEPS == 3:
        plan = [(0, [2, 6, 8]), (2, [32, 64, 224])]
    elif bits is None:
        plan = None
    else:
        plan = [(None, masks) for masks in split_even(bits, SWEEPS - 1)]
    second, partial = sweeps(coeffs, partial, plan)
    if bits is None:
        partial = lax.psum(partial, "region")
    first_damping = damp(partial[0])
    poly = partial[-1]
    for k in range(len(powers) - 2, -1, -1):
        poly = poly * first_damping + partial[1 + k]
    second_damping = damp(jnp.maximum(poly, 0.0))
    voltage = voltage + first_damping[:, None, None] * update
    step_update = second[-1]
    for k in range(terms - 2, -1, -1):
        step_update = step_update * first_damping[:, None, None] + second[k]
    voltage = voltage + second_damping[:, None, None] * step_update
    return voltage


def solution(mesh):
    in_specs = (
        P(None, "region", None),
        P("region", None),
        P("region", None),
        P("region", None),
        P("region"),
        P(),
        P(),
        P(),
        P(),
        P(None, None, "region"),
        P(),
        P("region"),
        P("region"),
        P("region"),
        P("region"),
        P("region", None),
    )
    out_specs = P(None, None, "region")
    return jax.shard_map(local, mesh=mesh, in_specs=in_specs, out_specs=out_specs, check_vma=False)
```

```python
import jax
import jax.numpy as jnp
from jax import lax
from jax.sharding import PartitionSpec as P

RW = 16
NEWTON = 2
SWEEPS = 3


trust_radius = 8.0
highest = lax.Precision.HIGHEST


def swap_pairs(count, offset, phase):
    pairs = []
    for low in range(count - offset):
        if (low // offset) % 2 == phase:
            pairs += [(low, low + offset), (low + offset, low)]
    return pairs


RINGS = (8, 4, 4, 2)


def sum_bits(axis):
    count = lax.axis_size(axis)
    if count & (count - 1):
        return None
    sizes = RINGS
    total = 1
    for size in sizes:
        total *= size
    if total != count:
        return [1 << b for b in range(count.bit_length() - 1)]
    near = {2: [1], 4: [1, 3], 8: [1, 2, 7]}
    masks, stride = [], 1
    for size in reversed(sizes):
        masks += [m * stride for m in near[size]]
        stride *= size
    return masks


def sum_rounds(value, axis, bits):
    count = lax.axis_size(axis)
    for bit in bits:
        value = value + lax.ppermute(value, axis, [(i, i ^ bit) for i in range(count)])
    return value


def split_even(items, parts):
    cuts = [len(items) * p // parts for p in range(parts + 1)]
    return [items[cuts[p] : cuts[p + 1]] for p in range(parts)]


def rotate(conduct, suscept, beside, axis):
    real_part = jnp.take(beside, 0, axis=axis)
    imag_part = jnp.take(beside, 1, axis=axis)
    return jnp.stack(
        [conduct * real_part - suscept * imag_part, suscept * real_part + conduct * imag_part],
        axis=axis,
    )


def local(
    features,
    line_mask,
    send_rows,
    attach_rows,
    tile_count,
    self_weight,
    neigh_weight,
    layer_bias,
    readout,
    load_table,
    scenario_profile,
    diag_admit,
    conductance,
    susceptance,
    load_coeff,
    region_inverse,
):
    scenarios, buses, width = features.shape
    neighbours, tile_size = send_rows.shape
    offsets = (1, -1, RW, -RW)
    count = lax.axis_size("region")
    me = lax.axis_index("region")
    routes, send_slots, recv_slots = [], [], []
    for offset, up, down in ((offsets[0], 0, 1), (offsets[2], 2, 3)):
        lower = (me // offset) % 2 == 0
        for phase in (0, 1):
            first = lower if phase == 0 else jnp.logical_not(lower)
            routes.append(swap_pairs(count, offset, phase))
            send_slots.append(jnp.where(first, up, down))
            recv_slots.append(jnp.where(first, down, up))
    send_slots = jnp.stack(send_slots)
    recv_slots = jnp.stack(recv_slots)
    bus_iota = lax.broadcasted_iota(jnp.int32, (neighbours, tile_size, buses), 2)
    live = lax.broadcasted_iota(jnp.int32, (neighbours, tile_size), 1) < tile_count[:, None]
    send_route = jnp.take(send_rows, send_slots, axis=0)
    live_route = jnp.take(live, send_slots, axis=0)
    attach_route = jnp.take(attach_rows, recv_slots, axis=0)
    pick = (send_route[:, :, None] == bus_iota) & live_route[:, :, None]
    place = attach_route[:, :, None] == bus_iota
    pick_half, pick_full = pick.astype(jnp.bfloat16), pick.astype(jnp.float32)
    place_half, place_full = place.astype(jnp.bfloat16), place.astype(jnp.float32)
    mask_half = line_mask.astype(jnp.bfloat16)
    mask_full = line_mask.astype(jnp.float32)
    pick_half, pick_full, place_half, place_full, mask_half, mask_full = lax.optimization_barrier(
        (pick_half, pick_full, place_half, place_full, mask_half, mask_full)
    )

    def exchange(tiles):
        return jnp.stack(
            [lax.ppermute(tiles[j], "region", routes[j]) for j in range(len(routes))]
        )

    hidden = features
    for number in range(self_weight.shape[0]):
        tiles = jnp.einsum(
            "ktb,sbh->ksth", pick_half, hidden, preferred_element_type=jnp.float32
        ).astype(jnp.bfloat16)
        incoming = exchange(tiles)
        inside = jnp.einsum("ij,sjh->sih", mask_half, hidden, preferred_element_type=jnp.float32)
        own = jnp.einsum(
            "sbh,hk->sbk", hidden, self_weight[number], preferred_element_type=jnp.float32
        )
        border = jnp.einsum(
            "ktb,ksth->sbh", place_half, incoming, preferred_element_type=jnp.float32
        )
        gathered = (0.25 * (inside + border)).astype(jnp.bfloat16)
        summed = (
            own
            + jnp.einsum(
                "sbh,hk->sbk", gathered, neigh_weight[number], preferred_element_type=jnp.float32
            )
            + layer_bias[number]
        )
        hidden = (hidden.astype(jnp.float32) + jax.nn.silu(summed)).astype(jnp.bfloat16)
    flat_start = jnp.array([1.0, 0.0], dtype=jnp.float32)[None, :, None]
    voltage = (
        jnp.einsum("sbh,ch->scb", hidden, readout, preferred_element_type=jnp.float32) + flat_start
    )
    choose = (
        scenario_profile[:, None]
        == lax.broadcasted_iota(jnp.int32, (scenarios, load_table.shape[0]), 1)
    ).astype(jnp.float32)
    injection = jnp.einsum("sp,pcb->scb", choose, load_table, precision=highest)
    bus_total = buses * lax.axis_size("region")

    def halo(values, payload=None):
        shape = values.shape
        flat = values.reshape((-1,) + shape[-2:])
        tiles = jnp.einsum("ktb,ncb->knct", pick_full, flat, precision=highest)
        rows = flat.shape[0]
        if payload is not None:
            cell = tiles.shape[-2] * tiles.shape[-1]
            packed = jnp.pad(payload.reshape(-1), (0, cell - payload.size))
            packed = packed.reshape((1, 1) + tiles.shape[-2:])
            packed = jnp.broadcast_to(packed, (tiles.shape[0], 1) + tiles.shape[-2:])
            tiles = jnp.concatenate([tiles, packed], axis=1)
        incoming = exchange(tiles)
        spread = jnp.einsum(
            "knct,ktb->ncb", incoming[:, :rows], place_full, precision=highest
        ).reshape(shape)
        if payload is None:
            return spread
        carried = incoming[:, rows].reshape(incoming.shape[0], -1)[:, : payload.size]
        return spread, carried.reshape((incoming.shape[0],) + payload.shape)

    def inside_sum(values):
        return jnp.einsum("ij,...cj->...ci", mask_full, values, precision=highest)

    def damp(squares):
        return jnp.minimum(1.0, trust_radius / jnp.sqrt(squares / (2 * bus_total) + 1e-06))

    def sweeps(residuals, partial, plan):
        count = residuals.shape[0]
        update = None
        for sweep_number in range(SWEEPS):
            forcing = -residuals
            if sweep_number > 0:
                carry, masks = plan[sweep_number - 1] if plan else (None, [])
                if carry is None:
                    arrived = halo(update)
                    if masks:
                        partial = sum_rounds(partial, "region", masks)
                        partial, arrived = lax.optimization_barrier((partial, arrived))
                else:
                    arrived, carried = halo(update, partial)
                    partial = sum_rounds(partial + carried[carry], "region", masks)
                forcing = forcing + rotate(conductance, susceptance, arrived, -2)
            forcing = forcing.reshape(count * scenarios, 2 * buses).astype(jnp.bfloat16)
            update = jnp.dot(forcing, region_inverse, preferred_element_type=jnp.float32)
            update = update.reshape(count, scenarios, 2, buses)
        return update, partial

    assert NEWTON == 2
    bits = sum_bits("region")
    beside = inside_sum(voltage) + halo(voltage)
    magnitude = voltage[:, 0:1] ** 2 + voltage[:, 1:2] ** 2
    residual = (
        diag_admit * voltage
        - rotate(conductance, susceptance, beside, 1)
        + load_coeff * magnitude * voltage
        - injection
    )
    partial = jnp.sum(residual * residual, axis=(1, 2))[None]
    update, partial = sweeps(residual[None], partial, None)
    update = update[0]
    extra = inside_sum(update) + halo(update)
    cross = 2.0 * (voltage[:, 0:1] * update[:, 0:1] + voltage[:, 1:2] * update[:, 1:2])
    square = update[:, 0:1] ** 2 + update[:, 1:2] ** 2
    coeffs = jnp.stack(
        [
            residual,
            diag_admit * update
            - rotate(conductance, susceptance, extra, 1)
            + load_coeff * (magnitude * update + cross * voltage),
            load_coeff * (cross * update + square * voltage),
            load_coeff * square * update,
        ]
    )
    terms = coeffs.shape[0]
    powers = [0.0] * (2 * terms - 1)
    for i in range(terms):
        for j in range(i, terms):
            product = jnp.sum(coeffs[i] * coeffs[j], axis=(1, 2))
            powers[i + j] = powers[i + j] + (product if i == j else 2.0 * product)
    partial = jnp.concatenate([partial, jnp.stack(powers)])
    if bits == [1, 2, 6, 8, 24, 32, 64, 224] and SWEEPS == 3:
        plan = [(0, [2, 6, 8]), (2, [32, 64, 224])]
    elif bits is None:
        plan = None
    else:
        plan = [(None, masks) for masks in split_even(bits, SWEEPS - 1)]
    second, partial = sweeps(coeffs, partial, plan)
    if bits is None:
        partial = lax.psum(partial, "region")
    first_damping = damp(partial[0])
    poly = partial[-1]
    for k in range(len(powers) - 2, -1, -1):
        poly = poly * first_damping + partial[1 + k]
    second_damping = damp(jnp.maximum(poly, 0.0))
    voltage = voltage + first_damping[:, None, None] * update
    step_update = second[-1]
    for k in range(terms - 2, -1, -1):
        step_update = step_update * first_damping[:, None, None] + second[k]
    voltage = voltage + second_damping[:, None, None] * step_update
    return voltage


def solution(mesh):
    in_specs = (
        P(None, "region", None),
        P("region", None),
        P("region", None),
        P("region", None),
        P("region"),
        P(),
        P(),
        P(),
        P(),
        P(None, None, "region"),
        P(),
        P("region"),
        P("region"),
        P("region"),
        P("region"),
        P("region", None),
    )
    out_specs = P(None, None, "region")
    return jax.shard_map(local, mesh=mesh, in_specs=in_specs, out_specs=out_specs, check_vma=False)
```

```python
import jax
import jax.numpy as jnp
from jax import lax
from jax.sharding import PartitionSpec as P

RW = 16
NEWTON = 2
SWEEPS = 3


trust_radius = 8.0
highest = lax.Precision.HIGHEST


def swap_pairs(count, offset, phase):
    pairs = []
    for low in range(count - offset):
        if (low // offset) % 2 == phase:
            pairs += [(low, low + offset), (low + offset, low)]
    return pairs


RINGS = (8, 4, 4, 2)


def sum_bits(axis):
    count = lax.axis_size(axis)
    if count & (count - 1):
        return None
    sizes = RINGS
    total = 1
    for size in sizes:
        total *= size
    if total != count:
        return [1 << b for b in range(count.bit_length() - 1)]
    near = {2: [1], 4: [1, 3], 8: [1, 2, 7]}
    masks, stride = [], 1
    for size in reversed(sizes):
        masks += [m * stride for m in near[size]]
        stride *= size
    return masks


def sum_rounds(value, axis, bits):
    count = lax.axis_size(axis)
    for bit in bits:
        value = value + lax.ppermute(value, axis, [(i, i ^ bit) for i in range(count)])
    return value


def split_even(items, parts):
    cuts = [len(items) * p // parts for p in range(parts + 1)]
    return [items[cuts[p] : cuts[p + 1]] for p in range(parts)]


def rotate(conduct, suscept, beside, axis):
    real_part = jnp.take(beside, 0, axis=axis)
    imag_part = jnp.take(beside, 1, axis=axis)
    return jnp.stack(
        [conduct * real_part - suscept * imag_part, suscept * real_part + conduct * imag_part],
        axis=axis,
    )


def local(
    features,
    line_mask,
    send_rows,
    attach_rows,
    tile_count,
    self_weight,
    neigh_weight,
    layer_bias,
    readout,
    load_table,
    scenario_profile,
    diag_admit,
    conductance,
    susceptance,
    load_coeff,
    region_inverse,
):
    scenarios, buses, width = features.shape
    neighbours, tile_size = send_rows.shape
    offsets = (1, -1, RW, -RW)
    count = lax.axis_size("region")
    me = lax.axis_index("region")
    routes, send_slots, recv_slots = [], [], []
    for offset, up, down in ((offsets[0], 0, 1), (offsets[2], 2, 3)):
        lower = (me // offset) % 2 == 0
        for phase in (0, 1):
            first = lower if phase == 0 else jnp.logical_not(lower)
            routes.append(swap_pairs(count, offset, phase))
            send_slots.append(jnp.where(first, up, down))
            recv_slots.append(jnp.where(first, down, up))
    send_slots = jnp.stack(send_slots)
    recv_slots = jnp.stack(recv_slots)
    bus_iota = lax.broadcasted_iota(jnp.int32, (neighbours, tile_size, buses), 2)
    live = lax.broadcasted_iota(jnp.int32, (neighbours, tile_size), 1) < tile_count[:, None]
    send_route = jnp.take(send_rows, send_slots, axis=0)
    live_route = jnp.take(live, send_slots, axis=0)
    attach_route = jnp.take(attach_rows, recv_slots, axis=0)
    pick = (send_route[:, :, None] == bus_iota) & live_route[:, :, None]
    place = attach_route[:, :, None] == bus_iota
    pick_half, pick_full = pick.astype(jnp.bfloat16), pick.astype(jnp.float32)
    place_half, place_full = place.astype(jnp.bfloat16), place.astype(jnp.float32)
    mask_half = line_mask.astype(jnp.bfloat16)
    mask_full = line_mask.astype(jnp.float32)

    def exchange(tiles):
        return jnp.stack(
            [lax.ppermute(tiles[j], "region", routes[j]) for j in range(len(routes))]
        )

    hidden = features
    for number in range(self_weight.shape[0]):
        tiles = jnp.einsum(
            "ktb,sbh->ksth", pick_half, hidden, preferred_element_type=jnp.float32
        ).astype(jnp.bfloat16)
        incoming = exchange(tiles)
        inside = jnp.einsum("ij,sjh->sih", mask_half, hidden, preferred_element_type=jnp.float32)
        own = jnp.einsum(
            "sbh,hk->sbk", hidden, self_weight[number], preferred_element_type=jnp.float32
        )
        border = jnp.einsum(
            "ktb,ksth->sbh", place_half, incoming, preferred_element_type=jnp.float32
        )
        gathered = (0.25 * (inside + border)).astype(jnp.bfloat16)
        summed = (
            own
            + jnp.einsum(
                "sbh,hk->sbk", gathered, neigh_weight[number], preferred_element_type=jnp.float32
            )
            + layer_bias[number]
        )
        hidden = (hidden.astype(jnp.float32) + jax.nn.silu(summed)).astype(jnp.bfloat16)
    flat_start = jnp.array([1.0, 0.0], dtype=jnp.float32)[None, :, None]
    voltage = (
        jnp.einsum("sbh,ch->scb", hidden, readout, preferred_element_type=jnp.float32) + flat_start
    )
    choose = (
        scenario_profile[:, None]
        == lax.broadcasted_iota(jnp.int32, (scenarios, load_table.shape[0]), 1)
    ).astype(jnp.float32)
    injection = jnp.einsum("sp,pcb->scb", choose, load_table, precision=highest)
    bus_total = buses * lax.axis_size("region")

    def halo(values, payload=None):
        shape = values.shape
        flat = values.reshape((-1,) + shape[-2:])
        tiles = jnp.einsum("ktb,ncb->knct", pick_full, flat, precision=highest)
        rows = flat.shape[0]
        if payload is not None:
            cell = tiles.shape[-2] * tiles.shape[-1]
            packed = jnp.pad(payload.reshape(-1), (0, cell - payload.size))
            packed = packed.reshape((1, 1) + tiles.shape[-2:])
            packed = jnp.broadcast_to(packed, (tiles.shape[0], 1) + tiles.shape[-2:])
            tiles = jnp.concatenate([tiles, packed], axis=1)
        incoming = exchange(tiles)
        spread = jnp.einsum(
            "knct,ktb->ncb", incoming[:, :rows], place_full, precision=highest
        ).reshape(shape)
        if payload is None:
            return spread
        carried = incoming[:, rows].reshape(incoming.shape[0], -1)[:, : payload.size]
        return spread, carried.reshape((incoming.shape[0],) + payload.shape)

    def inside_sum(values):
        return jnp.einsum("ij,...cj->...ci", mask_full, values, precision=highest)

    def damp(squares):
        return jnp.minimum(1.0, trust_radius / jnp.sqrt(squares / (2 * bus_total) + 1e-06))

    def sweeps(residuals, partial, plan):
        count = residuals.shape[0]

        def solve(forcing):
            forcing = forcing.reshape(count * scenarios, 2 * buses).astype(jnp.bfloat16)
            update = jnp.dot(forcing, region_inverse, preferred_element_type=jnp.float32)
            return update.reshape(count, scenarios, 2, buses)

        if plan is None:
            def body(_, update):
                arrived = halo(update)
                return solve(rotate(conductance, susceptance, arrived, -2) - residuals)

            return lax.fori_loop(1, SWEEPS, body, solve(-residuals)), partial
        update = None
        for sweep_number in range(SWEEPS):
            forcing = -residuals
            if sweep_number > 0:
                carry, masks = plan[sweep_number - 1] if plan else (None, [])
                if carry is None:
                    arrived = halo(update)
                    if masks:
                        partial = sum_rounds(partial, "region", masks)
                        partial, arrived = lax.optimization_barrier((partial, arrived))
                else:
                    arrived, carried = halo(update, partial)
                    partial = sum_rounds(partial + carried[carry], "region", masks)
                forcing = forcing + rotate(conductance, susceptance, arrived, -2)
            forcing = forcing.reshape(count * scenarios, 2 * buses).astype(jnp.bfloat16)
            update = jnp.dot(forcing, region_inverse, preferred_element_type=jnp.float32)
            update = update.reshape(count, scenarios, 2, buses)
        return update, partial

    assert NEWTON == 2
    bits = sum_bits("region")
    beside = inside_sum(voltage) + halo(voltage)
    magnitude = voltage[:, 0:1] ** 2 + voltage[:, 1:2] ** 2
    residual = (
        diag_admit * voltage
        - rotate(conductance, susceptance, beside, 1)
        + load_coeff * magnitude * voltage
        - injection
    )
    partial = jnp.sum(residual * residual, axis=(1, 2))[None]
    update, partial = sweeps(residual[None], partial, None)
    update = update[0]
    extra = inside_sum(update) + halo(update)
    cross = 2.0 * (voltage[:, 0:1] * update[:, 0:1] + voltage[:, 1:2] * update[:, 1:2])
    square = update[:, 0:1] ** 2 + update[:, 1:2] ** 2
    coeffs = jnp.stack(
        [
            residual,
            diag_admit * update
            - rotate(conductance, susceptance, extra, 1)
            + load_coeff * (magnitude * update + cross * voltage),
            load_coeff * (cross * update + square * voltage),
            load_coeff * square * update,
        ]
    )
    terms = coeffs.shape[0]
    powers = [0.0] * (2 * terms - 1)
    for i in range(terms):
        for j in range(i, terms):
            product = jnp.sum(coeffs[i] * coeffs[j], axis=(1, 2))
            powers[i + j] = powers[i + j] + (product if i == j else 2.0 * product)
    partial = jnp.concatenate([partial, jnp.stack(powers)])
    if bits == [1, 2, 6, 8, 24, 32, 64, 224] and SWEEPS == 3:
        plan = [(0, [2, 6, 8]), (2, [32, 64, 224])]
    elif bits is None:
        plan = None
    else:
        plan = [(None, masks) for masks in split_even(bits, SWEEPS - 1)]
    second, partial = sweeps(coeffs, partial, plan)
    if bits is None:
        partial = lax.psum(partial, "region")
    first_damping = damp(partial[0])
    poly = partial[-1]
    for k in range(len(powers) - 2, -1, -1):
        poly = poly * first_damping + partial[1 + k]
    second_damping = damp(jnp.maximum(poly, 0.0))
    voltage = voltage + first_damping[:, None, None] * update
    step_update = second[-1]
    for k in range(terms - 2, -1, -1):
        step_update = step_update * first_damping[:, None, None] + second[k]
    voltage = voltage + second_damping[:, None, None] * step_update
    return voltage


def solution(mesh):
    in_specs = (
        P(None, "region", None),
        P("region", None),
        P("region", None),
        P("region", None),
        P("region"),
        P(),
        P(),
        P(),
        P(),
        P(None, None, "region"),
        P(),
        P("region"),
        P("region"),
        P("region"),
        P("region"),
        P("region", None),
    )
    out_specs = P(None, None, "region")
    return jax.shard_map(local, mesh=mesh, in_specs=in_specs, out_specs=out_specs, check_vma=False)
```

```python
import jax
import jax.numpy as jnp
from jax import lax
from jax.sharding import PartitionSpec as P

RW = 16
NEWTON = 2
SWEEPS = 3


trust_radius = 8.0
highest = lax.Precision.HIGHEST


def swap_pairs(count, offset, phase):
    pairs = []
    for low in range(count - offset):
        if (low // offset) % 2 == phase:
            pairs += [(low, low + offset), (low + offset, low)]
    return pairs


RINGS = (8, 4, 4, 2)


def sum_bits(axis):
    count = lax.axis_size(axis)
    if count & (count - 1):
        return None
    sizes = RINGS
    total = 1
    for size in sizes:
        total *= size
    if total != count:
        return [1 << b for b in range(count.bit_length() - 1)]
    near = {2: [1], 4: [1, 3], 8: [1, 2, 7]}
    masks, stride = [], 1
    for size in reversed(sizes):
        masks += [m * stride for m in near[size]]
        stride *= size
    return masks


def sum_rounds(value, axis, bits):
    count = lax.axis_size(axis)
    for bit in bits:
        value = value + lax.ppermute(value, axis, [(i, i ^ bit) for i in range(count)])
    return value


def split_even(items, parts):
    cuts = [len(items) * p // parts for p in range(parts + 1)]
    return [items[cuts[p] : cuts[p + 1]] for p in range(parts)]


def rotate(conduct, suscept, beside, axis):
    real_part = jnp.take(beside, 0, axis=axis)
    imag_part = jnp.take(beside, 1, axis=axis)
    return jnp.stack(
        [conduct * real_part - suscept * imag_part, suscept * real_part + conduct * imag_part],
        axis=axis,
    )


def local(
    features,
    line_mask,
    send_rows,
    attach_rows,
    tile_count,
    self_weight,
    neigh_weight,
    layer_bias,
    readout,
    load_table,
    scenario_profile,
    diag_admit,
    conductance,
    susceptance,
    load_coeff,
    region_inverse,
):
    scenarios, buses, width = features.shape
    neighbours, tile_size = send_rows.shape
    offsets = (1, -1, RW, -RW)
    count = lax.axis_size("region")
    me = lax.axis_index("region")
    routes, send_slots, recv_slots = [], [], []
    for offset, up, down in ((offsets[2], 2, 3), (offsets[0], 0, 1)):
        lower = (me // offset) % 2 == 0
        for phase in (0, 1):
            first = lower if phase == 0 else jnp.logical_not(lower)
            routes.append(swap_pairs(count, offset, phase))
            send_slots.append(jnp.where(first, up, down))
            recv_slots.append(jnp.where(first, down, up))
    send_slots = jnp.stack(send_slots)
    recv_slots = jnp.stack(recv_slots)
    bus_iota = lax.broadcasted_iota(jnp.int32, (neighbours, tile_size, buses), 2)
    live = lax.broadcasted_iota(jnp.int32, (neighbours, tile_size), 1) < tile_count[:, None]
    send_route = jnp.take(send_rows, send_slots, axis=0)
    live_route = jnp.take(live, send_slots, axis=0)
    attach_route = jnp.take(attach_rows, recv_slots, axis=0)
    pick = (send_route[:, :, None] == bus_iota) & live_route[:, :, None]
    place = attach_route[:, :, None] == bus_iota
    pick_half, pick_full = pick.astype(jnp.bfloat16), pick.astype(jnp.float32)
    place_half, place_full = place.astype(jnp.bfloat16), place.astype(jnp.float32)
    mask_half = line_mask.astype(jnp.bfloat16)
    mask_full = line_mask.astype(jnp.float32)

    def exchange(tiles):
        return jnp.stack(
            [lax.ppermute(tiles[j], "region", routes[j]) for j in range(len(routes))]
        )

    hidden = features
    for number in range(self_weight.shape[0]):
        tiles = jnp.einsum(
            "ktb,sbh->ksth", pick_half, hidden, preferred_element_type=jnp.float32
        ).astype(jnp.bfloat16)
        incoming = exchange(tiles)
        inside = jnp.einsum("ij,sjh->sih", mask_half, hidden, preferred_element_type=jnp.float32)
        own = jnp.einsum(
            "sbh,hk->sbk", hidden, self_weight[number], preferred_element_type=jnp.float32
        )
        border = jnp.einsum(
            "ktb,ksth->sbh", place_half, incoming, preferred_element_type=jnp.float32
        )
        gathered = (0.25 * (inside + border)).astype(jnp.bfloat16)
        summed = (
            own
            + jnp.einsum(
                "sbh,hk->sbk", gathered, neigh_weight[number], preferred_element_type=jnp.float32
            )
            + layer_bias[number]
        )
        hidden = (hidden.astype(jnp.float32) + jax.nn.silu(summed)).astype(jnp.bfloat16)
    flat_start = jnp.array([1.0, 0.0], dtype=jnp.float32)[None, :, None]
    voltage = (
        jnp.einsum("sbh,ch->scb", hidden, readout, preferred_element_type=jnp.float32) + flat_start
    )
    choose = (
        scenario_profile[:, None]
        == lax.broadcasted_iota(jnp.int32, (scenarios, load_table.shape[0]), 1)
    ).astype(jnp.float32)
    injection = jnp.einsum("sp,pcb->scb", choose, load_table, precision=highest)
    bus_total = buses * lax.axis_size("region")

    def halo(values, payload=None):
        shape = values.shape
        flat = values.reshape((-1,) + shape[-2:])
        tiles = jnp.einsum("ktb,ncb->knct", pick_full, flat, precision=highest)
        rows = flat.shape[0]
        if payload is not None:
            cell = tiles.shape[-2] * tiles.shape[-1]
            packed = jnp.pad(payload.reshape(-1), (0, cell - payload.size))
            packed = packed.reshape((1, 1) + tiles.shape[-2:])
            packed = jnp.broadcast_to(packed, (tiles.shape[0], 1) + tiles.shape[-2:])
            tiles = jnp.concatenate([tiles, packed], axis=1)
        incoming = exchange(tiles)
        spread = jnp.einsum(
            "knct,ktb->ncb", incoming[:, :rows], place_full, precision=highest
        ).reshape(shape)
        if payload is None:
            return spread
        carried = incoming[:, rows].reshape(incoming.shape[0], -1)[:, : payload.size]
        return spread, carried.reshape((incoming.shape[0],) + payload.shape)

    def inside_sum(values):
        return jnp.einsum("ij,...cj->...ci", mask_full, values, precision=highest)

    def damp(squares):
        return jnp.minimum(1.0, trust_radius / jnp.sqrt(squares / (2 * bus_total) + 1e-06))

    def sweeps(residuals, partial, plan):
        count = residuals.shape[0]

        def solve(forcing):
            forcing = forcing.reshape(count * scenarios, 2 * buses).astype(jnp.bfloat16)
            update = jnp.dot(forcing, region_inverse, preferred_element_type=jnp.float32)
            return update.reshape(count, scenarios, 2, buses)

        if plan is None:
            def body(_, update):
                arrived = halo(update)
                return solve(rotate(conductance, susceptance, arrived, -2) - residuals)

            return lax.fori_loop(1, SWEEPS, body, solve(-residuals)), partial
        update = None
        for sweep_number in range(SWEEPS):
            forcing = -residuals
            if sweep_number > 0:
                carry, masks = plan[sweep_number - 1] if plan else (None, [])
                if carry is None:
                    arrived = halo(update)
                    if masks:
                        partial = sum_rounds(partial, "region", masks)
                        partial, arrived = lax.optimization_barrier((partial, arrived))
                else:
                    arrived, carried = halo(update, partial)
                    partial = sum_rounds(partial + carried[carry], "region", masks)
                forcing = forcing + rotate(conductance, susceptance, arrived, -2)
            forcing = forcing.reshape(count * scenarios, 2 * buses).astype(jnp.bfloat16)
            update = jnp.dot(forcing, region_inverse, preferred_element_type=jnp.float32)
            update = update.reshape(count, scenarios, 2, buses)
        return update, partial

    assert NEWTON == 2
    bits = sum_bits("region")
    beside = inside_sum(voltage) + halo(voltage)
    magnitude = voltage[:, 0:1] ** 2 + voltage[:, 1:2] ** 2
    residual = (
        diag_admit * voltage
        - rotate(conductance, susceptance, beside, 1)
        + load_coeff * magnitude * voltage
        - injection
    )
    partial = jnp.sum(residual * residual, axis=(1, 2))[None]
    update, partial = sweeps(residual[None], partial, None)
    update = update[0]
    extra = inside_sum(update) + halo(update)
    cross = 2.0 * (voltage[:, 0:1] * update[:, 0:1] + voltage[:, 1:2] * update[:, 1:2])
    square = update[:, 0:1] ** 2 + update[:, 1:2] ** 2
    coeffs = jnp.stack(
        [
            residual,
            diag_admit * update
            - rotate(conductance, susceptance, extra, 1)
            + load_coeff * (magnitude * update + cross * voltage),
            load_coeff * (cross * update + square * voltage),
            load_coeff * square * update,
        ]
    )
    terms = coeffs.shape[0]
    powers = [0.0] * (2 * terms - 1)
    for i in range(terms):
        for j in range(i, terms):
            product = jnp.sum(coeffs[i] * coeffs[j], axis=(1, 2))
            powers[i + j] = powers[i + j] + (product if i == j else 2.0 * product)
    partial = jnp.concatenate([partial, jnp.stack(powers)])
    if bits == [1, 2, 6, 8, 24, 32, 64, 224] and SWEEPS == 3:
        plan = [(2, [2, 6, 8]), (0, [32, 64, 224])]
    elif bits is None:
        plan = None
    else:
        plan = [(None, masks) for masks in split_even(bits, SWEEPS - 1)]
    second, partial = sweeps(coeffs, partial, plan)
    if bits is None:
        partial = lax.psum(partial, "region")
    first_damping = damp(partial[0])
    poly = partial[-1]
    for k in range(len(powers) - 2, -1, -1):
        poly = poly * first_damping + partial[1 + k]
    second_damping = damp(jnp.maximum(poly, 0.0))
    voltage = voltage + first_damping[:, None, None] * update
    step_update = second[-1]
    for k in range(terms - 2, -1, -1):
        step_update = step_update * first_damping[:, None, None] + second[k]
    voltage = voltage + second_damping[:, None, None] * step_update
    return voltage


def solution(mesh):
    in_specs = (
        P(None, "region", None),
        P("region", None),
        P("region", None),
        P("region", None),
        P("region"),
        P(),
        P(),
        P(),
        P(),
        P(None, None, "region"),
        P(),
        P("region"),
        P("region"),
        P("region"),
        P("region"),
        P("region", None),
    )
    out_specs = P(None, None, "region")
    return jax.shard_map(local, mesh=mesh, in_specs=in_specs, out_specs=out_specs, check_vma=False)
```

```python
import jax
import jax.numpy as jnp
from jax import lax
from jax.sharding import PartitionSpec as P

RW = 16
NEWTON = 2
SWEEPS = 3


trust_radius = 8.0
highest = lax.Precision.HIGHEST


def swap_pairs(count, offset, phase):
    pairs = []
    for low in range(count - offset):
        if (low // offset) % 2 == phase:
            pairs += [(low, low + offset), (low + offset, low)]
    return pairs


RINGS = (8, 4, 4, 2)


def sum_bits(axis):
    count = lax.axis_size(axis)
    if count & (count - 1):
        return None
    sizes = RINGS
    total = 1
    for size in sizes:
        total *= size
    if total != count:
        return [1 << b for b in range(count.bit_length() - 1)]
    near = {2: [1], 4: [1, 3], 8: [1, 2, 7]}
    masks, stride = [], 1
    for size in reversed(sizes):
        masks += [m * stride for m in near[size]]
        stride *= size
    return masks


def sum_rounds(value, axis, bits):
    count = lax.axis_size(axis)
    for bit in bits:
        value = value + lax.ppermute(value, axis, [(i, i ^ bit) for i in range(count)])
    return value


def split_even(items, parts):
    cuts = [len(items) * p // parts for p in range(parts + 1)]
    return [items[cuts[p] : cuts[p + 1]] for p in range(parts)]


def rotate(conduct, suscept, beside, axis):
    real_part = jnp.take(beside, 0, axis=axis)
    imag_part = jnp.take(beside, 1, axis=axis)
    return jnp.stack(
        [conduct * real_part - suscept * imag_part, suscept * real_part + conduct * imag_part],
        axis=axis,
    )


def local(
    features,
    line_mask,
    send_rows,
    attach_rows,
    tile_count,
    self_weight,
    neigh_weight,
    layer_bias,
    readout,
    load_table,
    scenario_profile,
    diag_admit,
    conductance,
    susceptance,
    load_coeff,
    region_inverse,
):
    scenarios, buses, width = features.shape
    neighbours, tile_size = send_rows.shape
    offsets = (1, -1, RW, -RW)
    count = lax.axis_size("region")
    me = lax.axis_index("region")
    routes, send_slots, recv_slots = [], [], []
    for offset, up, down in ((offsets[0], 0, 1), (offsets[2], 2, 3)):
        lower = (me // offset) % 2 == 0
        for phase in (0, 1):
            first = lower if phase == 0 else jnp.logical_not(lower)
            routes.append(swap_pairs(count, offset, phase))
            send_slots.append(jnp.where(first, up, down))
            recv_slots.append(jnp.where(first, down, up))
    send_slots = jnp.stack(send_slots)
    recv_slots = jnp.stack(recv_slots)
    bus_iota = lax.broadcasted_iota(jnp.int32, (neighbours, tile_size, buses), 2)
    live = lax.broadcasted_iota(jnp.int32, (neighbours, tile_size), 1) < tile_count[:, None]
    send_route = jnp.take(send_rows, send_slots, axis=0)
    live_route = jnp.take(live, send_slots, axis=0)
    attach_route = jnp.take(attach_rows, recv_slots, axis=0)
    pick = (send_route[:, :, None] == bus_iota) & live_route[:, :, None]
    place = attach_route[:, :, None] == bus_iota
    pick_half, pick_full = pick.astype(jnp.bfloat16), pick.astype(jnp.float32)
    place_half, place_full = place.astype(jnp.bfloat16), place.astype(jnp.float32)
    mask_half = line_mask.astype(jnp.bfloat16)
    mask_full = line_mask.astype(jnp.float32)

    def exchange(tiles, pieces=1):
        moved = []
        for j in range(len(routes)):
            slices = jnp.split(tiles[j], pieces, axis=0)
            got = [lax.ppermute(piece, "region", routes[j]) for piece in slices]
            moved.append(got[0] if pieces == 1 else jnp.concatenate(got, axis=0))
        return jnp.stack(moved)

    hidden = features
    for number in range(self_weight.shape[0]):
        tiles = jnp.einsum(
            "ktb,sbh->ksth", pick_half, hidden, preferred_element_type=jnp.float32
        ).astype(jnp.bfloat16)
        incoming = exchange(tiles, 2 if scenarios % 2 == 0 else 1)
        inside = jnp.einsum("ij,sjh->sih", mask_half, hidden, preferred_element_type=jnp.float32)
        own = jnp.einsum(
            "sbh,hk->sbk", hidden, self_weight[number], preferred_element_type=jnp.float32
        )
        border = jnp.einsum(
            "ktb,ksth->sbh", place_half, incoming, preferred_element_type=jnp.float32
        )
        gathered = (0.25 * (inside + border)).astype(jnp.bfloat16)
        summed = (
            own
            + jnp.einsum(
                "sbh,hk->sbk", gathered, neigh_weight[number], preferred_element_type=jnp.float32
            )
            + layer_bias[number]
        )
        hidden = (hidden.astype(jnp.float32) + jax.nn.silu(summed)).astype(jnp.bfloat16)
    flat_start = jnp.array([1.0, 0.0], dtype=jnp.float32)[None, :, None]
    voltage = (
        jnp.einsum("sbh,ch->scb", hidden, readout, preferred_element_type=jnp.float32) + flat_start
    )
    choose = (
        scenario_profile[:, None]
        == lax.broadcasted_iota(jnp.int32, (scenarios, load_table.shape[0]), 1)
    ).astype(jnp.float32)
    injection = jnp.einsum("sp,pcb->scb", choose, load_table, precision=highest)
    bus_total = buses * lax.axis_size("region")

    def halo(values, payload=None):
        shape = values.shape
        flat = values.reshape((-1,) + shape[-2:])
        tiles = jnp.einsum("ktb,ncb->knct", pick_full, flat, precision=highest)
        rows = flat.shape[0]
        if payload is not None:
            cell = tiles.shape[-2] * tiles.shape[-1]
            packed = jnp.pad(payload.reshape(-1), (0, cell - payload.size))
            packed = packed.reshape((1, 1) + tiles.shape[-2:])
            packed = jnp.broadcast_to(packed, (tiles.shape[0], 1) + tiles.shape[-2:])
            tiles = jnp.concatenate([tiles, packed], axis=1)
        incoming = exchange(tiles)
        spread = jnp.einsum(
            "knct,ktb->ncb", incoming[:, :rows], place_full, precision=highest
        ).reshape(shape)
        if payload is None:
            return spread
        carried = incoming[:, rows].reshape(incoming.shape[0], -1)[:, : payload.size]
        return spread, carried.reshape((incoming.shape[0],) + payload.shape)

    def inside_sum(values):
        return jnp.einsum("ij,...cj->...ci", mask_full, values, precision=highest)

    def damp(squares):
        return jnp.minimum(1.0, trust_radius / jnp.sqrt(squares / (2 * bus_total) + 1e-06))

    def sweeps(residuals, partial, plan):
        count = residuals.shape[0]

        def solve(forcing):
            forcing = forcing.reshape(count * scenarios, 2 * buses).astype(jnp.bfloat16)
            update = jnp.dot(forcing, region_inverse, preferred_element_type=jnp.float32)
            return update.reshape(count, scenarios, 2, buses)

        if plan is None:
            def body(_, update):
                arrived = halo(update)
                return solve(rotate(conductance, susceptance, arrived, -2) - residuals)

            return lax.fori_loop(1, SWEEPS, body, solve(-residuals)), partial
        update = None
        for sweep_number in range(SWEEPS):
            forcing = -residuals
            if sweep_number > 0:
                carry, masks = plan[sweep_number - 1] if plan else (None, [])
                if carry is None:
                    arrived = halo(update)
                    if masks:
                        partial = sum_rounds(partial, "region", masks)
                        partial, arrived = lax.optimization_barrier((partial, arrived))
                else:
                    arrived, carried = halo(update, partial)
                    partial = sum_rounds(partial + carried[carry], "region", masks)
                forcing = forcing + rotate(conductance, susceptance, arrived, -2)
            forcing = forcing.reshape(count * scenarios, 2 * buses).astype(jnp.bfloat16)
            update = jnp.dot(forcing, region_inverse, preferred_element_type=jnp.float32)
            update = update.reshape(count, scenarios, 2, buses)
        return update, partial

    assert NEWTON == 2
    bits = sum_bits("region")
    beside = inside_sum(voltage) + halo(voltage)
    magnitude = voltage[:, 0:1] ** 2 + voltage[:, 1:2] ** 2
    residual = (
        diag_admit * voltage
        - rotate(conductance, susceptance, beside, 1)
        + load_coeff * magnitude * voltage
        - injection
    )
    partial = jnp.sum(residual * residual, axis=(1, 2))[None]
    update, partial = sweeps(residual[None], partial, None)
    update = update[0]
    extra = inside_sum(update) + halo(update)
    cross = 2.0 * (voltage[:, 0:1] * update[:, 0:1] + voltage[:, 1:2] * update[:, 1:2])
    square = update[:, 0:1] ** 2 + update[:, 1:2] ** 2
    coeffs = jnp.stack(
        [
            residual,
            diag_admit * update
            - rotate(conductance, susceptance, extra, 1)
            + load_coeff * (magnitude * update + cross * voltage),
            load_coeff * (cross * update + square * voltage),
            load_coeff * square * update,
        ]
    )
    terms = coeffs.shape[0]
    powers = [0.0] * (2 * terms - 1)
    for i in range(terms):
        for j in range(i, terms):
            product = jnp.sum(coeffs[i] * coeffs[j], axis=(1, 2))
            powers[i + j] = powers[i + j] + (product if i == j else 2.0 * product)
    partial = jnp.concatenate([partial, jnp.stack(powers)])
    if bits == [1, 2, 6, 8, 24, 32, 64, 224] and SWEEPS == 3:
        plan = [(0, [2, 6, 8]), (2, [32, 64, 224])]
    elif bits is None:
        plan = None
    else:
        plan = [(None, masks) for masks in split_even(bits, SWEEPS - 1)]
    second, partial = sweeps(coeffs, partial, plan)
    if bits is None:
        partial = lax.psum(partial, "region")
    first_damping = damp(partial[0])
    poly = partial[-1]
    for k in range(len(powers) - 2, -1, -1):
        poly = poly * first_damping + partial[1 + k]
    second_damping = damp(jnp.maximum(poly, 0.0))
    voltage = voltage + first_damping[:, None, None] * update
    step_update = second[-1]
    for k in range(terms - 2, -1, -1):
        step_update = step_update * first_damping[:, None, None] + second[k]
    voltage = voltage + second_damping[:, None, None] * step_update
    return voltage


def solution(mesh):
    in_specs = (
        P(None, "region", None),
        P("region", None),
        P("region", None),
        P("region", None),
        P("region"),
        P(),
        P(),
        P(),
        P(),
        P(None, None, "region"),
        P(),
        P("region"),
        P("region"),
        P("region"),
        P("region"),
        P("region", None),
    )
    out_specs = P(None, None, "region")
    return jax.shard_map(local, mesh=mesh, in_specs=in_specs, out_specs=out_specs, check_vma=False)
```

```python
import jax
import jax.numpy as jnp
from jax import lax
from jax.sharding import PartitionSpec as P

RW = 16
NEWTON = 2
SWEEPS = 3


trust_radius = 8.0
highest = lax.Precision.HIGHEST


def swap_pairs(count, offset, phase):
    pairs = []
    for low in range(count - offset):
        if (low // offset) % 2 == phase:
            pairs += [(low, low + offset), (low + offset, low)]
    return pairs


RINGS = (8, 4, 4, 2)


def sum_bits(axis):
    count = lax.axis_size(axis)
    if count & (count - 1):
        return None
    sizes = RINGS
    total = 1
    for size in sizes:
        total *= size
    if total != count:
        return [1 << b for b in range(count.bit_length() - 1)]
    near = {2: [1], 4: [1, 3], 8: [1, 2, 7]}
    masks, stride = [], 1
    for size in reversed(sizes):
        masks += [m * stride for m in near[size]]
        stride *= size
    return masks


def sum_rounds(value, axis, bits):
    count = lax.axis_size(axis)
    for bit in bits:
        group = bit if isinstance(bit, tuple) else (bit,)
        moved = [lax.ppermute(value, axis, [(i, i ^ m) for i in range(count)]) for m in group]
        for got in moved:
            value = value + got
    return value


def split_even(items, parts):
    cuts = [len(items) * p // parts for p in range(parts + 1)]
    return [items[cuts[p] : cuts[p + 1]] for p in range(parts)]


def rotate(conduct, suscept, beside, axis):
    real_part = jnp.take(beside, 0, axis=axis)
    imag_part = jnp.take(beside, 1, axis=axis)
    return jnp.stack(
        [conduct * real_part - suscept * imag_part, suscept * real_part + conduct * imag_part],
        axis=axis,
    )


def local(
    features,
    line_mask,
    send_rows,
    attach_rows,
    tile_count,
    self_weight,
    neigh_weight,
    layer_bias,
    readout,
    load_table,
    scenario_profile,
    diag_admit,
    conductance,
    susceptance,
    load_coeff,
    region_inverse,
):
    scenarios, buses, width = features.shape
    neighbours, tile_size = send_rows.shape
    offsets = (1, -1, RW, -RW)
    count = lax.axis_size("region")
    me = lax.axis_index("region")
    routes, send_slots, recv_slots = [], [], []
    for offset, up, down in ((offsets[0], 0, 1), (offsets[2], 2, 3)):
        lower = (me // offset) % 2 == 0
        for phase in (0, 1):
            first = lower if phase == 0 else jnp.logical_not(lower)
            routes.append(swap_pairs(count, offset, phase))
            send_slots.append(jnp.where(first, up, down))
            recv_slots.append(jnp.where(first, down, up))
    send_slots = jnp.stack(send_slots)
    recv_slots = jnp.stack(recv_slots)
    bus_iota = lax.broadcasted_iota(jnp.int32, (neighbours, tile_size, buses), 2)
    live = lax.broadcasted_iota(jnp.int32, (neighbours, tile_size), 1) < tile_count[:, None]
    send_route = jnp.take(send_rows, send_slots, axis=0)
    live_route = jnp.take(live, send_slots, axis=0)
    attach_route = jnp.take(attach_rows, recv_slots, axis=0)
    pick = (send_route[:, :, None] == bus_iota) & live_route[:, :, None]
    place = attach_route[:, :, None] == bus_iota
    pick_half, pick_full = pick.astype(jnp.bfloat16), pick.astype(jnp.float32)
    place_half, place_full = place.astype(jnp.bfloat16), place.astype(jnp.float32)
    mask_half = line_mask.astype(jnp.bfloat16)
    mask_full = line_mask.astype(jnp.float32)

    def exchange(tiles):
        return jnp.stack(
            [lax.ppermute(tiles[j], "region", routes[j]) for j in range(len(routes))]
        )

    hidden = features
    for number in range(self_weight.shape[0]):
        tiles = jnp.einsum(
            "ktb,sbh->ksth", pick_half, hidden, preferred_element_type=jnp.float32
        ).astype(jnp.bfloat16)
        incoming = exchange(tiles)
        inside = jnp.einsum("ij,sjh->sih", mask_half, hidden, preferred_element_type=jnp.float32)
        own = jnp.einsum(
            "sbh,hk->sbk", hidden, self_weight[number], preferred_element_type=jnp.float32
        )
        border = jnp.einsum(
            "ktb,ksth->sbh", place_half, incoming, preferred_element_type=jnp.float32
        )
        gathered = (0.25 * (inside + border)).astype(jnp.bfloat16)
        summed = (
            own
            + jnp.einsum(
                "sbh,hk->sbk", gathered, neigh_weight[number], preferred_element_type=jnp.float32
            )
            + layer_bias[number]
        )
        hidden = (hidden.astype(jnp.float32) + jax.nn.silu(summed)).astype(jnp.bfloat16)
    flat_start = jnp.array([1.0, 0.0], dtype=jnp.float32)[None, :, None]
    voltage = (
        jnp.einsum("sbh,ch->scb", hidden, readout, preferred_element_type=jnp.float32) + flat_start
    )
    choose = (
        scenario_profile[:, None]
        == lax.broadcasted_iota(jnp.int32, (scenarios, load_table.shape[0]), 1)
    ).astype(jnp.float32)
    injection = jnp.einsum("sp,pcb->scb", choose, load_table, precision=highest)
    bus_total = buses * lax.axis_size("region")

    def halo(values, payload=None):
        shape = values.shape
        flat = values.reshape((-1,) + shape[-2:])
        tiles = jnp.einsum("ktb,ncb->knct", pick_full, flat, precision=highest)
        rows = flat.shape[0]
        if payload is not None:
            cell = tiles.shape[-2] * tiles.shape[-1]
            packed = jnp.pad(payload.reshape(-1), (0, cell - payload.size))
            packed = packed.reshape((1, 1) + tiles.shape[-2:])
            packed = jnp.broadcast_to(packed, (tiles.shape[0], 1) + tiles.shape[-2:])
            tiles = jnp.concatenate([tiles, packed], axis=1)
        incoming = exchange(tiles)
        spread = jnp.einsum(
            "knct,ktb->ncb", incoming[:, :rows], place_full, precision=highest
        ).reshape(shape)
        if payload is None:
            return spread
        carried = incoming[:, rows].reshape(incoming.shape[0], -1)[:, : payload.size]
        return spread, carried.reshape((incoming.shape[0],) + payload.shape)

    def inside_sum(values):
        return jnp.einsum("ij,...cj->...ci", mask_full, values, precision=highest)

    def damp(squares):
        return jnp.minimum(1.0, trust_radius / jnp.sqrt(squares / (2 * bus_total) + 1e-06))

    def sweeps(residuals, partial, plan):
        count = residuals.shape[0]
        update = None
        for sweep_number in range(SWEEPS):
            forcing = -residuals
            if sweep_number > 0:
                carry, masks = plan[sweep_number - 1] if plan else (None, [])
                if carry is None:
                    arrived = halo(update)
                    if masks:
                        partial = sum_rounds(partial, "region", masks)
                        partial, arrived = lax.optimization_barrier((partial, arrived))
                else:
                    arrived, carried = halo(update, partial)
                    partial = sum_rounds(partial + carried[carry], "region", masks)
                forcing = forcing + rotate(conductance, susceptance, arrived, -2)
            forcing = forcing.reshape(count * scenarios, 2 * buses).astype(jnp.bfloat16)
            update = jnp.dot(forcing, region_inverse, preferred_element_type=jnp.float32)
            update = update.reshape(count, scenarios, 2, buses)
        return update, partial

    assert NEWTON == 2
    bits = sum_bits("region")
    beside = inside_sum(voltage) + halo(voltage)
    magnitude = voltage[:, 0:1] ** 2 + voltage[:, 1:2] ** 2
    residual = (
        diag_admit * voltage
        - rotate(conductance, susceptance, beside, 1)
        + load_coeff * magnitude * voltage
        - injection
    )
    partial = jnp.sum(residual * residual, axis=(1, 2))[None]
    update, partial = sweeps(residual[None], partial, None)
    update = update[0]
    extra = inside_sum(update) + halo(update)
    cross = 2.0 * (voltage[:, 0:1] * update[:, 0:1] + voltage[:, 1:2] * update[:, 1:2])
    square = update[:, 0:1] ** 2 + update[:, 1:2] ** 2
    coeffs = jnp.stack(
        [
            residual,
            diag_admit * update
            - rotate(conductance, susceptance, extra, 1)
            + load_coeff * (magnitude * update + cross * voltage),
            load_coeff * (cross * update + square * voltage),
            load_coeff * square * update,
        ]
    )
    terms = coeffs.shape[0]
    powers = [0.0] * (2 * terms - 1)
    for i in range(terms):
        for j in range(i, terms):
            product = jnp.sum(coeffs[i] * coeffs[j], axis=(1, 2))
            powers[i + j] = powers[i + j] + (product if i == j else 2.0 * product)
    partial = jnp.concatenate([partial, jnp.stack(powers)])
    if bits == [1, 2, 6, 8, 24, 32, 64, 224] and SWEEPS == 3:
        plan = [(0, [(2, 4, 6), 8]), (2, [(32, 64, 96, 128, 160, 192, 224)])]
    elif bits is None:
        plan = None
    else:
        plan = [(None, masks) for masks in split_even(bits, SWEEPS - 1)]
    second, partial = sweeps(coeffs, partial, plan)
    if bits is None:
        partial = lax.psum(partial, "region")
    first_damping = damp(partial[0])
    poly = partial[-1]
    for k in range(len(powers) - 2, -1, -1):
        poly = poly * first_damping + partial[1 + k]
    second_damping = damp(jnp.maximum(poly, 0.0))
    voltage = voltage + first_damping[:, None, None] * update
    step_update = second[-1]
    for k in range(terms - 2, -1, -1):
        step_update = step_update * first_damping[:, None, None] + second[k]
    voltage = voltage + second_damping[:, None, None] * step_update
    return voltage


def solution(mesh):
    in_specs = (
        P(None, "region", None),
        P("region", None),
        P("region", None),
        P("region", None),
        P("region"),
        P(),
        P(),
        P(),
        P(),
        P(None, None, "region"),
        P(),
        P("region"),
        P("region"),
        P("region"),
        P("region"),
        P("region", None),
    )
    out_specs = P(None, None, "region")
    return jax.shard_map(local, mesh=mesh, in_specs=in_specs, out_specs=out_specs, check_vma=False)
```

```python
import jax
import jax.numpy as jnp
from jax import lax
from jax.sharding import PartitionSpec as P

RW = 16
NEWTON = 2
SWEEPS = 3


trust_radius = 8.0
highest = lax.Precision.HIGHEST


def swap_pairs(count, offset, phase):
    pairs = []
    for low in range(count - offset):
        if (low // offset) % 2 == phase:
            pairs += [(low, low + offset), (low + offset, low)]
    return pairs


RINGS = (8, 4, 4, 2)


def sum_bits(axis):
    count = lax.axis_size(axis)
    if count & (count - 1):
        return None
    sizes = RINGS
    total = 1
    for size in sizes:
        total *= size
    if total != count:
        return [1 << b for b in range(count.bit_length() - 1)]
    near = {2: [1], 4: [1, 3], 8: [1, 2, 7]}
    masks, stride = [], 1
    for size in reversed(sizes):
        masks += [m * stride for m in near[size]]
        stride *= size
    return masks


def sum_rounds(value, axis, bits):
    count = lax.axis_size(axis)
    for bit in bits:
        value = value + lax.ppermute(value, axis, [(i, i ^ bit) for i in range(count)])
    return value


def split_even(items, parts):
    cuts = [len(items) * p // parts for p in range(parts + 1)]
    return [items[cuts[p] : cuts[p + 1]] for p in range(parts)]


def rotate(conduct, suscept, beside, axis):
    real_part = jnp.take(beside, 0, axis=axis)
    imag_part = jnp.take(beside, 1, axis=axis)
    return jnp.stack(
        [conduct * real_part - suscept * imag_part, suscept * real_part + conduct * imag_part],
        axis=axis,
    )


def local(
    features,
    line_mask,
    send_rows,
    attach_rows,
    tile_count,
    self_weight,
    neigh_weight,
    layer_bias,
    readout,
    load_table,
    scenario_profile,
    diag_admit,
    conductance,
    susceptance,
    load_coeff,
    region_inverse,
):
    scenarios, buses, width = features.shape
    neighbours, tile_size = send_rows.shape
    offsets = (1, -1, RW, -RW)
    count = lax.axis_size("region")
    me = lax.axis_index("region")
    routes, send_slots, recv_slots = [], [], []
    for offset, up, down in ((offsets[0], 0, 1), (offsets[2], 2, 3)):
        lower = (me // offset) % 2 == 0
        for phase in (0, 1):
            first = lower if phase == 0 else jnp.logical_not(lower)
            routes.append(swap_pairs(count, offset, phase))
            send_slots.append(jnp.where(first, up, down))
            recv_slots.append(jnp.where(first, down, up))
    send_slots = jnp.stack(send_slots)
    recv_slots = jnp.stack(recv_slots)
    bus_iota = lax.broadcasted_iota(jnp.int32, (neighbours, tile_size, buses), 2)
    live = lax.broadcasted_iota(jnp.int32, (neighbours, tile_size), 1) < tile_count[:, None]
    send_route = jnp.take(send_rows, send_slots, axis=0)
    live_route = jnp.take(live, send_slots, axis=0)
    attach_route = jnp.take(attach_rows, recv_slots, axis=0)
    pick = (send_route[:, :, None] == bus_iota) & live_route[:, :, None]
    place = attach_route[:, :, None] == bus_iota
    pick_half, pick_full = pick.astype(jnp.bfloat16), pick.astype(jnp.float32)
    place_half, place_full = place.astype(jnp.bfloat16), place.astype(jnp.float32)
    mask_half = line_mask.astype(jnp.bfloat16)
    mask_full = line_mask.astype(jnp.float32)

    def exchange(tiles):
        return jnp.stack(
            [lax.ppermute(tiles[j], "region", routes[j]) for j in range(len(routes))]
        )

    hidden = features
    for number in range(self_weight.shape[0]):
        tiles = jnp.einsum(
            "ktb,sbh->ksth", pick_half, hidden, preferred_element_type=jnp.float32
        ).astype(jnp.bfloat16)
        incoming = exchange(tiles)
        inside = jnp.einsum("ij,sjh->sih", mask_half, hidden, preferred_element_type=jnp.float32)
        own = jnp.einsum(
            "sbh,hk->sbk", hidden, self_weight[number], preferred_element_type=jnp.float32
        )
        arrived = jnp.transpose(incoming, (1, 0, 2, 3)).reshape(scenarios, -1, width)
        border = jnp.einsum(
            "rb,srh->sbh",
            place_half.reshape(-1, buses),
            arrived,
            preferred_element_type=jnp.float32,
        )
        gathered = (0.25 * (inside + border)).astype(jnp.bfloat16)
        summed = (
            own
            + jnp.einsum(
                "sbh,hk->sbk", gathered, neigh_weight[number], preferred_element_type=jnp.float32
            )
            + layer_bias[number]
        )
        hidden = (hidden.astype(jnp.float32) + jax.nn.silu(summed)).astype(jnp.bfloat16)
    flat_start = jnp.array([1.0, 0.0], dtype=jnp.float32)[None, :, None]
    voltage = (
        jnp.einsum("sbh,ch->scb", hidden, readout, preferred_element_type=jnp.float32) + flat_start
    )
    choose = (
        scenario_profile[:, None]
        == lax.broadcasted_iota(jnp.int32, (scenarios, load_table.shape[0]), 1)
    ).astype(jnp.float32)
    injection = jnp.einsum("sp,pcb->scb", choose, load_table, precision=highest)
    bus_total = buses * lax.axis_size("region")

    def halo(values, payload=None):
        shape = values.shape
        flat = values.reshape((-1,) + shape[-2:])
        tiles = jnp.einsum("ktb,ncb->knct", pick_full, flat, precision=highest)
        rows = flat.shape[0]
        if payload is not None:
            cell = tiles.shape[-2] * tiles.shape[-1]
            packed = jnp.pad(payload.reshape(-1), (0, cell - payload.size))
            packed = packed.reshape((1, 1) + tiles.shape[-2:])
            packed = jnp.broadcast_to(packed, (tiles.shape[0], 1) + tiles.shape[-2:])
            tiles = jnp.concatenate([tiles, packed], axis=1)
        incoming = exchange(tiles)
        spread = jnp.einsum(
            "knct,ktb->ncb", incoming[:, :rows], place_full, precision=highest
        ).reshape(shape)
        if payload is None:
            return spread
        carried = incoming[:, rows].reshape(incoming.shape[0], -1)[:, : payload.size]
        return spread, carried.reshape((incoming.shape[0],) + payload.shape)

    def inside_sum(values):
        return jnp.einsum("ij,...cj->...ci", mask_full, values, precision=highest)

    def damp(squares):
        return jnp.minimum(1.0, trust_radius / jnp.sqrt(squares / (2 * bus_total) + 1e-06))

    def sweeps(residuals, partial, plan):
        count = residuals.shape[0]
        update = None
        for sweep_number in range(SWEEPS):
            forcing = -residuals
            if sweep_number > 0:
                carry, masks = plan[sweep_number - 1] if plan else (None, [])
                if carry is None:
                    arrived = halo(update)
                    if masks:
                        partial = sum_rounds(partial, "region", masks)
                        partial, arrived = lax.optimization_barrier((partial, arrived))
                else:
                    arrived, carried = halo(update, partial)
                    partial = sum_rounds(partial + carried[carry], "region", masks)
                forcing = forcing + rotate(conductance, susceptance, arrived, -2)
            forcing = forcing.reshape(count * scenarios, 2 * buses).astype(jnp.bfloat16)
            update = jnp.dot(forcing, region_inverse, preferred_element_type=jnp.float32)
            update = update.reshape(count, scenarios, 2, buses)
        return update, partial

    assert NEWTON == 2
    bits = sum_bits("region")
    beside = inside_sum(voltage) + halo(voltage)
    magnitude = voltage[:, 0:1] ** 2 + voltage[:, 1:2] ** 2
    residual = (
        diag_admit * voltage
        - rotate(conductance, susceptance, beside, 1)
        + load_coeff * magnitude * voltage
        - injection
    )
    partial = jnp.sum(residual * residual, axis=(1, 2))[None]
    update, partial = sweeps(residual[None], partial, None)
    update = update[0]
    extra = inside_sum(update) + halo(update)
    cross = 2.0 * (voltage[:, 0:1] * update[:, 0:1] + voltage[:, 1:2] * update[:, 1:2])
    square = update[:, 0:1] ** 2 + update[:, 1:2] ** 2
    coeffs = jnp.stack(
        [
            residual,
            diag_admit * update
            - rotate(conductance, susceptance, extra, 1)
            + load_coeff * (magnitude * update + cross * voltage),
            load_coeff * (cross * update + square * voltage),
            load_coeff * square * update,
        ]
    )
    terms = coeffs.shape[0]
    powers = [0.0] * (2 * terms - 1)
    for i in range(terms):
        for j in range(i, terms):
            product = jnp.sum(coeffs[i] * coeffs[j], axis=(1, 2))
            powers[i + j] = powers[i + j] + (product if i == j else 2.0 * product)
    partial = jnp.concatenate([partial, jnp.stack(powers)])
    if bits == [1, 2, 6, 8, 24, 32, 64, 224] and SWEEPS == 3:
        plan = [(0, [2, 6, 8]), (2, [32, 64, 224])]
    elif bits is None:
        plan = None
    else:
        plan = [(None, masks) for masks in split_even(bits, SWEEPS - 1)]
    second, partial = sweeps(coeffs, partial, plan)
    if bits is None:
        partial = lax.psum(partial, "region")
    first_damping = damp(partial[0])
    poly = partial[-1]
    for k in range(len(powers) - 2, -1, -1):
        poly = poly * first_damping + partial[1 + k]
    second_damping = damp(jnp.maximum(poly, 0.0))
    voltage = voltage + first_damping[:, None, None] * update
    step_update = second[-1]
    for k in range(terms - 2, -1, -1):
        step_update = step_update * first_damping[:, None, None] + second[k]
    voltage = voltage + second_damping[:, None, None] * step_update
    return voltage


def solution(mesh):
    in_specs = (
        P(None, "region", None),
        P("region", None),
        P("region", None),
        P("region", None),
        P("region"),
        P(),
        P(),
        P(),
        P(),
        P(None, None, "region"),
        P(),
        P("region"),
        P("region"),
        P("region"),
        P("region"),
        P("region", None),
    )
    out_specs = P(None, None, "region")
    return jax.shard_map(local, mesh=mesh, in_specs=in_specs, out_specs=out_specs, check_vma=False)
```

```python
import jax
import jax.numpy as jnp
from jax import lax
from jax.sharding import PartitionSpec as P

RW = 16
NEWTON = 2
SWEEPS = 3


trust_radius = 8.0
highest = lax.Precision.HIGHEST


def swap_pairs(count, offset, phase):
    pairs = []
    for low in range(count - offset):
        if (low // offset) % 2 == phase:
            pairs += [(low, low + offset), (low + offset, low)]
    return pairs


RINGS = (8, 4, 4, 2)


def sum_bits(axis):
    count = lax.axis_size(axis)
    if count & (count - 1):
        return None
    sizes = RINGS
    total = 1
    for size in sizes:
        total *= size
    if total != count:
        return [1 << b for b in range(count.bit_length() - 1)]
    near = {2: [1], 4: [1, 3], 8: [1, 2, 7]}
    masks, stride = [], 1
    for size in reversed(sizes):
        masks += [m * stride for m in near[size]]
        stride *= size
    return masks


def sum_rounds(value, axis, bits):
    count = lax.axis_size(axis)
    for bit in bits:
        value = value + lax.ppermute(value, axis, [(i, i ^ bit) for i in range(count)])
    return value


def split_even(items, parts):
    cuts = [len(items) * p // parts for p in range(parts + 1)]
    return [items[cuts[p] : cuts[p + 1]] for p in range(parts)]


def rotate(conduct, suscept, beside, axis):
    real_part = jnp.take(beside, 0, axis=axis)
    imag_part = jnp.take(beside, 1, axis=axis)
    return jnp.stack(
        [conduct * real_part - suscept * imag_part, suscept * real_part + conduct * imag_part],
        axis=axis,
    )


def local(
    features,
    line_mask,
    send_rows,
    attach_rows,
    tile_count,
    self_weight,
    neigh_weight,
    layer_bias,
    readout,
    load_table,
    scenario_profile,
    diag_admit,
    conductance,
    susceptance,
    load_coeff,
    region_inverse,
):
    scenarios, buses, width = features.shape
    neighbours, tile_size = send_rows.shape
    offsets = (1, -1, RW, -RW)
    count = lax.axis_size("region")
    me = lax.axis_index("region")
    routes, send_slots, recv_slots = [], [], []
    for offset, up, down in ((offsets[0], 0, 1), (offsets[2], 2, 3)):
        lower = (me // offset) % 2 == 0
        for phase in (0, 1):
            first = lower if phase == 0 else jnp.logical_not(lower)
            routes.append(swap_pairs(count, offset, phase))
            send_slots.append(jnp.where(first, up, down))
            recv_slots.append(jnp.where(first, down, up))
    send_slots = jnp.stack(send_slots)
    recv_slots = jnp.stack(recv_slots)
    bus_iota = lax.broadcasted_iota(jnp.int32, (neighbours, tile_size, buses), 2)
    live = lax.broadcasted_iota(jnp.int32, (neighbours, tile_size), 1) < tile_count[:, None]
    send_route = jnp.take(send_rows, send_slots, axis=0)
    live_route = jnp.take(live, send_slots, axis=0)
    attach_route = jnp.take(attach_rows, recv_slots, axis=0)
    pick = (send_route[:, :, None] == bus_iota) & live_route[:, :, None]
    place = attach_route[:, :, None] == bus_iota
    pick_half, pick_full = pick.astype(jnp.bfloat16), pick.astype(jnp.float32)
    place_half, place_full = place.astype(jnp.bfloat16), place.astype(jnp.float32)
    mask_half = line_mask.astype(jnp.bfloat16)
    mask_full = line_mask.astype(jnp.float32)

    def exchange(tiles):
        return jnp.stack(
            [lax.ppermute(tiles[j], "region", routes[j]) for j in range(len(routes))]
        )

    hidden = features
    for number in range(self_weight.shape[0]):
        tiles = jnp.einsum(
            "ktb,sbh->ksth", pick_half, hidden, preferred_element_type=jnp.float32
        ).astype(jnp.bfloat16)
        incoming = exchange(tiles)
        inside = jnp.einsum("ij,sjh->sih", mask_half, hidden, preferred_element_type=jnp.float32)
        own = jnp.einsum(
            "sbh,hk->sbk", hidden, self_weight[number], preferred_element_type=jnp.float32
        )
        border = jnp.einsum(
            "ktb,ksth->sbh", place_half, incoming, preferred_element_type=jnp.float32
        )
        gathered = (0.25 * (inside + border)).astype(jnp.bfloat16)
        summed = (
            own
            + jnp.einsum(
                "sbh,hk->sbk", gathered, neigh_weight[number], preferred_element_type=jnp.float32
            )
            + layer_bias[number]
        )
        hidden = (hidden.astype(jnp.float32) + jax.nn.silu(summed)).astype(jnp.bfloat16)
    flat_start = jnp.array([1.0, 0.0], dtype=jnp.float32)[None, :, None]
    voltage = (
        jnp.einsum("sbh,ch->scb", hidden, readout, preferred_element_type=jnp.float32) + flat_start
    )
    choose = (
        scenario_profile[:, None]
        == lax.broadcasted_iota(jnp.int32, (scenarios, load_table.shape[0]), 1)
    ).astype(jnp.float32)
    injection = jnp.einsum("sp,pcb->scb", choose, load_table, precision=highest)
    bus_total = buses * lax.axis_size("region")

    def halo(values, payload=None):
        shape = values.shape
        flat = values.reshape((-1,) + shape[-2:])
        tiles = jnp.einsum("ktb,ncb->knct", pick_full, flat, precision=highest)
        rows = flat.shape[0]
        if payload is not None:
            cell = tiles.shape[-2] * tiles.shape[-1]
            packed = jnp.pad(payload.reshape(-1), (0, cell - payload.size))
            packed = packed.reshape((1, 1) + tiles.shape[-2:])
            packed = jnp.broadcast_to(packed, (tiles.shape[0], 1) + tiles.shape[-2:])
            tiles = jnp.concatenate([tiles, packed], axis=1)
        incoming = exchange(tiles)
        spread = jnp.einsum(
            "knct,ktb->ncb", incoming[:, :rows], place_full, precision=highest
        ).reshape(shape)
        if payload is None:
            return spread
        carried = incoming[:, rows].reshape(incoming.shape[0], -1)[:, : payload.size]
        return spread, carried.reshape((incoming.shape[0],) + payload.shape)

    def inside_sum(values):
        return jnp.einsum("ij,...cj->...ci", mask_full, values, precision=highest)

    def damp(squares):
        return jnp.minimum(1.0, trust_radius / jnp.sqrt(squares / (2 * bus_total) + 1e-06))

    def sweeps(residuals, partial, plan):
        count = residuals.shape[0]
        update = None
        for sweep_number in range(SWEEPS):
            forcing = -residuals
            if sweep_number > 0:
                carry, masks = plan[sweep_number - 1] if plan else (None, [])
                if carry is None:
                    arrived = halo(update)
                    if masks:
                        partial = sum_rounds(partial, "region", masks)
                        partial, arrived = lax.optimization_barrier((partial, arrived))
                else:
                    arrived, carried = halo(update, partial)
                    partial = sum_rounds(partial + carried[carry], "region", masks)
                forcing = forcing + rotate(conductance, susceptance, arrived, -2)
            forcing = forcing.reshape(count * scenarios, 2 * buses).astype(jnp.bfloat16)
            update = jnp.dot(forcing, region_inverse, preferred_element_type=jnp.float32)
            update = update.reshape(count, scenarios, 2, buses)
        return update, partial

    assert NEWTON == 2
    bits = sum_bits("region")
    beside = inside_sum(voltage) + halo(voltage)
    magnitude = voltage[:, 0:1] ** 2 + voltage[:, 1:2] ** 2
    residual = (
        diag_admit * voltage
        - rotate(conductance, susceptance, beside, 1)
        + load_coeff * magnitude * voltage
        - injection
    )
    partial = jnp.sum(residual * residual, axis=(1, 2))[None]
    update, partial = sweeps(residual[None], partial, None)
    update = update[0]
    extra = inside_sum(update) + halo(update)
    cross = 2.0 * (voltage[:, 0:1] * update[:, 0:1] + voltage[:, 1:2] * update[:, 1:2])
    square = update[:, 0:1] ** 2 + update[:, 1:2] ** 2
    coeffs = jnp.stack(
        [
            residual,
            diag_admit * update
            - rotate(conductance, susceptance, extra, 1)
            + load_coeff * (magnitude * update + cross * voltage),
            load_coeff * (cross * update + square * voltage),
            load_coeff * square * update,
        ]
    )
    terms = coeffs.shape[0]
    powers = [0.0] * (2 * terms - 1)
    for i in range(terms):
        for j in range(i, terms):
            product = jnp.sum(coeffs[i] * coeffs[j], axis=(1, 2))
            powers[i + j] = powers[i + j] + (product if i == j else 2.0 * product)
    partial = jnp.concatenate([partial, jnp.stack(powers)])
    if bits == [1, 2, 6, 8, 24, 32, 64, 224] and SWEEPS == 3:
        plan = [(0, []), (2, [2, 6, 8, 32, 64, 224])]
    elif bits is None:
        plan = None
    else:
        plan = [(None, masks) for masks in split_even(bits, SWEEPS - 1)]
    second, partial = sweeps(coeffs, partial, plan)
    if bits is None:
        partial = lax.psum(partial, "region")
    first_damping = damp(partial[0])
    poly = partial[-1]
    for k in range(len(powers) - 2, -1, -1):
        poly = poly * first_damping + partial[1 + k]
    second_damping = damp(jnp.maximum(poly, 0.0))
    voltage = voltage + first_damping[:, None, None] * update
    step_update = second[-1]
    for k in range(terms - 2, -1, -1):
        step_update = step_update * first_damping[:, None, None] + second[k]
    voltage = voltage + second_damping[:, None, None] * step_update
    return voltage


def solution(mesh):
    in_specs = (
        P(None, "region", None),
        P("region", None),
        P("region", None),
        P("region", None),
        P("region"),
        P(),
        P(),
        P(),
        P(),
        P(None, None, "region"),
        P(),
        P("region"),
        P("region"),
        P("region"),
        P("region"),
        P("region", None),
    )
    out_specs = P(None, None, "region")
    return jax.shard_map(local, mesh=mesh, in_specs=in_specs, out_specs=out_specs, check_vma=False)
```
